512 devices in a mesh: tiles: 32 (over z, core), chan: 16 (over y, x).
Axes of the slice: x: 4, y: 4, z: 16, core: 2. Of those that a mesh axis runs over, the one named last changes fastest.
Arguments:
- atmos_state: bfloat16 [256, 192, 256], P('tiles', 'chan'), may hold values from -6 to 6
- ocean_state: bfloat16 [256, 128, 256], P('tiles', 'chan'), may hold values from -6 to 6
- atmos_weight: bfloat16 [9, 192, 192], P(None, 'chan'), may hold values from -0.15625 to 0.15625
- ocean_weight: bfloat16 [9, 128, 128], P(None, 'chan'), may hold values from -0.1875 to 0.1875
- couple_weight: bfloat16 [128, 192], P('chan'), may hold values from -0.4375 to 0.4375
- sea_mask: int32 [256], replicated, may hold values from 0 to 1, as said below
- neighbours: int32 [256, 4], replicated, may hold values from 0 to 255, as said below
- rotations: int32 [256, 4], replicated, may hold values from 0 to 7
Outputs:
- atmos_next: bfloat16 [256, 192, 256], P('tiles', 'chan')
- ocean_next: bfloat16 [192, 128, 256], P('tiles', 'chan')
The draws below stay inside these ranges and needn't reach their ends.
Inputs may be any that keep to these rules, and one draw needn't show every extreme that they name: `sea_mask`: exactly 192 of the 256 entries are 1; the tiles of blocks 2k and 2k + 1 of 8 tiles hold exactly 12 sea tiles together, and each such block holds between 4 and 8. neighbours[t, s] lies in the block of 8 tiles that holds t, or in the block just before or just after it, cyclically over the 32 blocks.
All inputs are finite; a program needn't handle non-finite values.
Results may differ from the reference program's by a relative error of at most 0.0034.
Values may be sent and summed in bfloat16 or wider, within the bound.
No kernel may reach another device: no remote copies, remote signals or barrier semaphores. Data moves between devices by JAX's collectives and lax.ppermute only.
A program may use at most 64 MiB of HBM per device.

```python
import jax
import jax.numpy as jnp
from jax import lax

A_CH = 192
O_CH = 128
SIDE = 16
TPD = 8
OPD = 6
TILES = 256
OCEAN_TILES = 192
N_TILES = 32


def draw_sea_mask(key, part):
    key_shift = jax.random.fold_in(key, 11)
    key_order = jax.random.fold_in(key, 12)
    blocks = TILES // TPD
    pairs = blocks // 2
    shifts = jax.random.randint(key_shift, (pairs,), -(TPD // 4), TPD // 4 + 1).astype(jnp.int32)
    counts = jnp.stack([OPD + shifts, OPD - shifts], axis=1).reshape(blocks).astype(jnp.int32)
    tile_ids = jnp.arange(TILES, dtype=jnp.int32)
    block_ids = tile_ids // TPD
    scores = block_ids * TILES + jax.random.permutation(key_order, TILES).astype(jnp.int32)
    order = jnp.argsort(scores, stable=True).astype(jnp.int32)
    places = jnp.zeros((TILES,), jnp.int32).at[order].set(tile_ids)
    within = places - block_ids * TPD
    return (within < counts[block_ids]).astype(jnp.int32)


def draw_neighbours(key, part):
    key_step = jax.random.fold_in(key, 21)
    key_pick = jax.random.fold_in(key, 22)
    blocks = TILES // TPD
    tile_ids = jnp.arange(TILES, dtype=jnp.int32)
    step_block = jax.random.randint(key_step, (TILES, 4), -1, 2).astype(jnp.int32)
    target_block = ((tile_ids // TPD)[:, None] + step_block) % blocks
    return (target_block * TPD + jax.random.randint(key_pick, (TILES, 4), 0, TPD)).astype(jnp.int32)


def set_ends(values, rng, low, top_value):
    shape = values.shape
    spot = [jax.random.randint(jax.random.fold_in(rng, axis), (), 0, shape[axis]) for axis in range(len(shape))]
    values = values.at[tuple(spot)].set(low)
    longest = shape.index(max(shape))
    spot[longest] = (spot[longest] + 1) % shape[longest]
    return values.at[tuple(spot)].set(top_value)


def block_levels(stream_key, shape, shards, smallest, top_value):
    gain = 1.0
    for dim, shards_of in shards:
        draws = jax.random.uniform(jax.random.fold_in(jax.random.fold_in(stream_key, 6), dim), (shards_of,), jnp.float32, smallest / len(shards), top_value / len(shards))
        gain = gain * jnp.repeat(jnp.exp(draws), shape[dim] // shards_of).reshape((-1,) + (1,) * (len(shape) - 1 - dim))
    return gain


def gaussian(key, dims, deviation, limit, pieces=(), held_as=jnp.bfloat16):
    drawn = jax.random.normal(key, dims, jnp.float32) * deviation
    if len(pieces) > 0:
        drawn = block_levels(key, dims, pieces, -0.22, 0.18) * drawn
    return jnp.clip(drawn, min=-limit, max=limit).astype(held_as)


def setup_inputs(seed: int = 0) -> dict:
    arg_keys = jax.random.split(jax.random.key(seed), 9)
    return {
        "atmos_state": gaussian(arg_keys[0], (TILES, A_CH, SIDE * SIDE), 1.0, 6.0, ((0, 32), (1, 16))),
        "ocean_state": gaussian(arg_keys[1], (TILES, O_CH, SIDE * SIDE), 1.0, 6.0, ((0, 32), (1, 16))),
        "atmos_weight": gaussian(arg_keys[2], (9, A_CH, A_CH), (9 * A_CH) ** -0.5, 0.15625, ((1, 16),)),
        "ocean_weight": gaussian(arg_keys[3], (9, O_CH, O_CH), (9 * O_CH) ** -0.5, 0.1875, ((1, 16),)),
        "couple_weight": gaussian(arg_keys[4], (O_CH, A_CH), A_CH ** -0.5, 0.4375, ((0, 16),)),
        "sea_mask": draw_sea_mask(jax.random.fold_in(arg_keys[8], 71), 0),
        "neighbours": draw_neighbours(jax.random.fold_in(arg_keys[8], 71), 0),
        "rotations": set_ends(jax.random.randint(arg_keys[7], (TILES, 4), 0, 8), jax.random.fold_in(arg_keys[7], 1), 0, 7).astype(jnp.int32),
    }


def edge_set(tile_field):
    tile_count, chan_count = tile_field.shape[0], tile_field.shape[1]
    tile_grid = tile_field.reshape(tile_count, chan_count, SIDE, SIDE)
    return jnp.stack([tile_grid[:, :, 0, :], tile_grid[:, :, :, SIDE - 1], tile_grid[:, :, SIDE - 1, :], tile_grid[:, :, :, 0]], axis=2)


def pick_rims(edge_strips, adjacent, turn_codes):
    picked = edge_strips[adjacent]
    side_index = (turn_codes % 4).astype(jnp.int32)
    chosen = picked[:, :, :, 0, :]
    for edge_id in range(1, 4):
        chosen = jnp.where((side_index == edge_id)[:, :, None, None], picked[:, :, :, edge_id, :], chosen)
    return jnp.where((turn_codes >= 4)[:, :, None, None], chosen[..., ::-1], chosen)


def pad_tile(tile_field, rim_cells):
    tile_count, chan_count = tile_field.shape[0], tile_field.shape[1]
    tile_grid = tile_field.reshape(tile_count, chan_count, SIDE, SIDE)
    upper_row = jnp.pad(rim_cells[:, 0], ((0, 0), (0, 0), (1, 1)))[:, :, None, :]
    bottom = jnp.pad(rim_cells[:, 2], ((0, 0), (0, 0), (1, 1)))[:, :, None, :]
    middle = jnp.concatenate([rim_cells[:, 3][:, :, :, None], tile_grid, rim_cells[:, 1][:, :, :, None]], axis=3)
    assembled = jnp.concatenate([upper_row, middle, bottom], axis=2).reshape(tile_count, chan_count, (SIDE + 2) * (SIDE + 2))
    return jnp.pad(assembled, ((0, 0), (0, 0), (0, 2)))


def conv_sum(padded, weight):
    row_width = SIDE + 2
    out_span = SIDE * row_width
    accum = jnp.zeros((padded.shape[0], weight.shape[1], out_span), jnp.float32)
    for tap_index in range(9):
        offset = (tap_index // 3) * row_width + tap_index % 3
        accum = accum + jnp.einsum("oc,bcp->bop", weight[tap_index].astype(jnp.float32), padded[:, :, offset:offset + out_span].astype(jnp.float32))
    return accum


def trim_columns(accum):
    tile_count, chan_count = accum.shape[0], accum.shape[1]
    return accum.reshape(tile_count, chan_count, SIDE, SIDE + 2)[:, :, :, :SIDE].reshape(tile_count, chan_count, SIDE * SIDE)


def reference(atmos_state, ocean_state, atmos_weight, ocean_weight, couple_weight, sea_mask, neighbours, rotations):
    sea_field = ocean_state * sea_mask.astype(ocean_state.dtype)[:, None, None]
    atmos_edges = edge_set(atmos_state)
    sea_edges = edge_set(sea_field)

    def atmos_block(block_index):
        first_tile = block_index * TPD
        tile_field = lax.dynamic_slice_in_dim(atmos_state, first_tile, TPD, 0)
        adjacent = lax.dynamic_slice_in_dim(neighbours, first_tile, TPD, 0)
        turn_codes = lax.dynamic_slice_in_dim(rotations, first_tile, TPD, 0)
        accum = conv_sum(pad_tile(tile_field, pick_rims(atmos_edges, adjacent, turn_codes)), atmos_weight)
        return (tile_field.astype(jnp.float32) + jax.nn.gelu(trim_columns(accum), approximate=True)).astype(jnp.bfloat16)

    atmos_next = lax.map(atmos_block, jnp.arange(TILES // TPD, dtype=jnp.int32)).reshape(atmos_state.shape)

    sea_flags = sea_mask.astype(jnp.int32)
    sea_rank = (jnp.cumsum(sea_flags) - 1).astype(jnp.int32)
    rank_spots = jnp.where(sea_flags == 1, sea_rank, OCEAN_TILES).astype(jnp.int32)
    tile_of_rank = jnp.zeros((OCEAN_TILES,), jnp.int32).at[rank_spots].set(jnp.arange(TILES, dtype=jnp.int32), mode="drop")
    row_ids = jnp.arange(OCEAN_TILES, dtype=jnp.int32)
    row_ranks = (row_ids // (2 * OPD)) * (2 * OPD) + 2 * (row_ids % OPD) + (row_ids // OPD) % 2
    chosen_tiles = tile_of_rank[row_ranks.astype(jnp.int32)]

    def ocean_block(block_index):
        tiles_now = lax.dynamic_slice_in_dim(chosen_tiles, block_index * OPD, OPD, 0)
        own_state = ocean_state[tiles_now]
        rim_cells = pick_rims(sea_edges, neighbours[tiles_now], rotations[tiles_now])
        mixed = trim_columns(conv_sum(pad_tile(own_state, rim_cells), ocean_weight))
        forcing = atmos_next[tiles_now]
        mixed = mixed + jnp.einsum("oc,bcp->bop", couple_weight.astype(jnp.float32), forcing.astype(jnp.float32))
        return (own_state.astype(jnp.float32) + jax.nn.gelu(mixed, approximate=True)).astype(jnp.bfloat16)

    ocean_next = lax.map(ocean_block, jnp.arange(N_TILES, dtype=jnp.int32)).reshape(OCEAN_TILES, O_CH, SIDE * SIDE)
    return (atmos_next, ocean_next)
```

```python
import jax
import jax.numpy as jnp
from jax import lax
from jax.sharding import PartitionSpec as P

SIDE = 16


def padded_2(cells, sides, width):
    for axis, dim in sides:
        count = lax.axis_size(axis)
        head = lax.slice_in_dim(cells, 0, width, axis=dim)
        tail = lax.slice_in_dim(cells, cells.shape[dim] - width, cells.shape[dim], axis=dim)
        cells = jnp.concatenate(
            [
                lax.ppermute(tail, axis, [(i, (i + 1) % count) for i in range(count)]),
                cells,
                lax.ppermute(head, axis, [((i + 1) % count, i) for i in range(count)]),
            ],
            axis=dim,
        )
    return cells


def partner(value, axis, distance):
    mask = 2**distance
    pairs = [(source, source ^ mask) for source in range(lax.axis_size(axis))]
    return lax.ppermute(value, axis, pairs)


def edge_set(tile_field):
    tile_count, chan_count = (tile_field.shape[0], tile_field.shape[1])
    tile_grid = tile_field.reshape(tile_count, chan_count, SIDE, SIDE)
    return jnp.stack(
        [
            tile_grid[:, :, 0, :],
            tile_grid[:, :, :, SIDE - 1],
            tile_grid[:, :, SIDE - 1, :],
            tile_grid[:, :, :, 0],
        ],
        axis=2,
    )


def pick_rims(edge_strips, adjacent, turn_codes):
    picked = edge_strips[adjacent]
    side_index = turn_codes % 4
    chosen = picked[:, :, :, 0, :]
    for edge_id in range(1, 4):
        chosen = jnp.where(
            (side_index == edge_id)[:, :, None, None], picked[:, :, :, edge_id, :], chosen
        )
    return jnp.where((turn_codes >= 4)[:, :, None, None], chosen[..., ::-1], chosen)


def pad_tile(tile_field, rim_cells):
    tile_count, chan_count = (tile_field.shape[0], tile_field.shape[1])
    tile_grid = tile_field.reshape(tile_count, chan_count, SIDE, SIDE)
    upper_row = jnp.pad(rim_cells[:, 0], ((0, 0), (0, 0), (1, 1)))[:, :, None, :]
    bottom = jnp.pad(rim_cells[:, 2], ((0, 0), (0, 0), (1, 1)))[:, :, None, :]
    middle = jnp.concatenate(
        [rim_cells[:, 3][:, :, :, None], tile_grid, rim_cells[:, 1][:, :, :, None]], axis=3
    )
    assembled = jnp.concatenate([upper_row, middle, bottom], axis=2).reshape(
        tile_count, chan_count, (SIDE + 2) * (SIDE + 2)
    )
    return jnp.pad(assembled, ((0, 0), (0, 0), (0, 2)))


def trim_columns(accum):
    tile_count, chan_count = (accum.shape[0], accum.shape[1])
    return accum.reshape(tile_count, chan_count, SIDE, SIDE + 2)[:, :, :, :SIDE].reshape(
        tile_count, chan_count, SIDE * SIDE
    )


def conv_step(weight, accum, piece):
    row_width = SIDE + 2
    out_span = SIDE * row_width
    for tap_index in range(9):
        offset = tap_index // 3 * row_width + tap_index % 3
        accum = accum + jnp.einsum(
            "oc,bcp->bop",
            weight[tap_index],
            piece[:, :, offset : offset + out_span],
            preferred_element_type=jnp.float32,
        )
    return accum


def gather_rows(pieces):
    flat = jnp.concatenate([piece.reshape(-1) for piece in pieces])
    rows = flat.reshape(-1, SIDE * SIDE)
    gathered = lax.all_gather(rows, "chan", axis=0, tiled=False)
    groups = gathered.shape[0]
    gathered = gathered.reshape(groups, -1)
    parts = []
    offset = 0
    for piece in pieces:
        size = piece.size
        part = gathered[:, offset : offset + size].reshape((groups,) + piece.shape)
        parts.append(part)
        offset += size
    return parts


def merge_chans(part, chan_dim):
    moved = jnp.moveaxis(part, 0, chan_dim)
    shape = moved.shape
    return moved.reshape(shape[:chan_dim] + (shape[chan_dim] * shape[chan_dim + 1],) + shape[chan_dim + 2 :])


def local(
    atmos_state,
    ocean_state,
    atmos_weight,
    ocean_weight,
    couple_weight,
    sea_mask,
    neighbours,
    rotations,
):
    per_dev = atmos_state.shape[0]
    atmos_local = atmos_state.shape[1]
    ocean_local = ocean_state.shape[1]
    groups = lax.axis_size("tiles")
    tile_group = lax.axis_index("tiles")
    first_tile = tile_group * per_dev
    per_owner = per_dev * 3 // 4
    ocean_total = per_owner * groups
    counts = jnp.sum(sea_mask.reshape(groups, per_dev), axis=1)
    starts = jnp.cumsum(counts) - counts
    sea_rank = jnp.cumsum(sea_mask) - 1
    rank_spots = jnp.where(sea_mask == 1, sea_rank, ocean_total)
    tile_of_rank = (
        jnp.zeros((ocean_total,), jnp.int32)
        .at[rank_spots]
        .set(jnp.arange(sea_mask.shape[0], dtype=jnp.int32), mode="drop")
    )
    my_first = starts[tile_group]
    my_last = my_first + counts[tile_group]
    parity = tile_group % 2
    pair_base = tile_group // 2 * 2 * per_owner
    slot_ids = jnp.arange(per_owner, dtype=jnp.int32)
    ranks_send = pair_base + 2 * slot_ids + (1 - parity)
    ranks_own = pair_base + 2 * slot_ids + parity
    send_tile = jnp.clip(tile_of_rank[ranks_send] - first_tile, 0, per_dev - 1)
    own_tile = jnp.clip(tile_of_rank[ranks_own] - first_tile, 0, per_dev - 1)
    from_here = (ranks_own >= my_first) & (ranks_own < my_last)

    own_ocean = jnp.where(
        from_here[:, None, None], ocean_state[own_tile], partner(ocean_state[send_tile], "tiles", 0)
    )

    sea_here = lax.dynamic_slice_in_dim(sea_mask, first_tile, per_dev, 0)
    sea_field = ocean_state * sea_here.astype(jnp.bfloat16)[:, None, None]
    edge_strips = jnp.concatenate([edge_set(atmos_state), edge_set(sea_field)], axis=1)
    widened = padded_2(edge_strips.reshape(per_dev, -1), (("tiles", 0),), per_dev)
    widened = widened.reshape(3 * per_dev, atmos_local + ocean_local, 4, SIDE)
    adjacent = lax.dynamic_slice_in_dim(neighbours, first_tile, per_dev, 0)
    turn_codes = lax.dynamic_slice_in_dim(rotations, first_tile, per_dev, 0)
    local_adjacent = (adjacent // per_dev - tile_group + 1) % groups * per_dev + adjacent % per_dev
    rim_cells = pick_rims(widened, local_adjacent, turn_codes)

    early = 2 * SIDE
    atmos_int, atmos_rims, ocean_head = gather_rows(
        [atmos_state, rim_cells[:, :, :atmos_local], own_ocean[:, :, :early]]
    )
    atmos_pad = pad_tile(merge_chans(atmos_int, 1), merge_chans(atmos_rims, 2))
    atmos_start = jnp.zeros((per_dev, atmos_weight.shape[1], SIDE * (SIDE + 2)), jnp.float32)
    atmos_accum = conv_step(atmos_weight, atmos_start, atmos_pad)
    atmos_next = (
        atmos_state.astype(jnp.float32) + jax.nn.gelu(trim_columns(atmos_accum), approximate=True)
    ).astype(jnp.bfloat16)

    sea_width = ocean_local * 4 * SIDE
    late_block = jnp.concatenate(
        [atmos_next.reshape(per_dev, -1), rim_cells[:, :, atmos_local:].reshape(per_dev, -1)], axis=1
    )
    late_own = jnp.where(
        from_here[:, None], late_block[own_tile], partner(late_block[send_tile], "tiles", 0)
    )
    forcing = late_own[:, : late_block.shape[1] - sea_width].reshape(per_owner, atmos_local, SIDE * SIDE)
    own_rims = late_own[:, late_block.shape[1] - sea_width :].reshape(per_owner, 4, ocean_local, SIDE)

    ocean_tail, ocean_rims, force_parts = gather_rows([own_ocean[:, :, early:], own_rims, forcing])
    ocean_full = jnp.concatenate([merge_chans(ocean_head, 1), merge_chans(ocean_tail, 1)], axis=2)
    ocean_pad = pad_tile(ocean_full, merge_chans(ocean_rims, 2))
    force_all = merge_chans(force_parts, 1)
    conv_start = jnp.zeros((per_owner, ocean_weight.shape[1], SIDE * (SIDE + 2)), jnp.float32)
    conv_accum = conv_step(ocean_weight, conv_start, ocean_pad)
    couple_accum = jnp.einsum(
        "oc,bcp->bop", couple_weight, force_all, preferred_element_type=jnp.float32
    )
    mixed = trim_columns(conv_accum) + couple_accum
    ocean_next = (own_ocean.astype(jnp.float32) + jax.nn.gelu(mixed, approximate=True)).astype(
        jnp.bfloat16
    )
    return (atmos_next, ocean_next)


def solution(mesh):
    placed = (
        P("tiles", "chan", None),
        P("tiles", "chan", None),
        P(None, "chan", None),
        P(None, "chan", None),
        P("chan", None),
        P(),
        P(),
        P(),
    )
    return jax.shard_map(
        local,
        mesh=mesh,
        in_specs=placed,
        out_specs=(P("tiles", "chan", None), P("tiles", "chan", None)),
        check_vma=False,
    )
```

```python
import jax
import jax.numpy as jnp
from jax import lax
from jax.sharding import PartitionSpec as P

SIDE = 16


def padded_2(cells, sides, width):
    for axis, dim in sides:
        count = lax.axis_size(axis)
        head = lax.slice_in_dim(cells, 0, width, axis=dim)
        tail = lax.slice_in_dim(cells, cells.shape[dim] - width, cells.shape[dim], axis=dim)
        cells = jnp.concatenate(
            [
                lax.ppermute(tail, axis, [(i, (i + 1) % count) for i in range(count)]),
                cells,
                lax.ppermute(head, axis, [((i + 1) % count, i) for i in range(count)]),
            ],
            axis=dim,
        )
    return cells


def partner(value, axis, distance):
    mask = 2**distance
    pairs = [(source, source ^ mask) for source in range(lax.axis_size(axis))]
    return lax.ppermute(value, axis, pairs)


def edge_set(tile_field):
    tile_count, chan_count = (tile_field.shape[0], tile_field.shape[1])
    tile_grid = tile_field.reshape(tile_count, chan_count, SIDE, SIDE)
    return jnp.stack(
        [
            tile_grid[:, :, 0, :],
            tile_grid[:, :, :, SIDE - 1],
            tile_grid[:, :, SIDE - 1, :],
            tile_grid[:, :, :, 0],
        ],
        axis=2,
    )


def pick_rims(edge_strips, adjacent, turn_codes):
    picked = edge_strips[adjacent]
    side_index = turn_codes % 4
    chosen = picked[:, :, :, 0, :]
    for edge_id in range(1, 4):
        chosen = jnp.where(
            (side_index == edge_id)[:, :, None, None], picked[:, :, :, edge_id, :], chosen
        )
    return jnp.where((turn_codes >= 4)[:, :, None, None], chosen[..., ::-1], chosen)


def pad_tile(tile_field, rim_cells):
    tile_count, chan_count = (tile_field.shape[0], tile_field.shape[1])
    tile_grid = tile_field.reshape(tile_count, chan_count, SIDE, SIDE)
    upper_row = jnp.pad(rim_cells[:, 0], ((0, 0), (0, 0), (1, 1)))[:, :, None, :]
    bottom = jnp.pad(rim_cells[:, 2], ((0, 0), (0, 0), (1, 1)))[:, :, None, :]
    middle = jnp.concatenate(
        [rim_cells[:, 3][:, :, :, None], tile_grid, rim_cells[:, 1][:, :, :, None]], axis=3
    )
    assembled = jnp.concatenate([upper_row, middle, bottom], axis=2).reshape(
        tile_count, chan_count, (SIDE + 2) * (SIDE + 2)
    )
    return jnp.pad(assembled, ((0, 0), (0, 0), (0, 2)))


def trim_columns(accum):
    tile_count, chan_count = (accum.shape[0], accum.shape[1])
    return accum.reshape(tile_count, chan_count, SIDE, SIDE + 2)[:, :, :, :SIDE].reshape(
        tile_count, chan_count, SIDE * SIDE
    )


def conv_step(weight, accum, piece):
    row_width = SIDE + 2
    out_span = SIDE * row_width
    for tap_index in range(9):
        offset = tap_index // 3 * row_width + tap_index % 3
        accum = accum + jnp.einsum(
            "oc,bcp->bop",
            weight[tap_index],
            piece[:, :, offset : offset + out_span],
            preferred_element_type=jnp.float32,
        )
    return accum


def gather_rows(pieces):
    flat = jnp.concatenate([piece.reshape(-1) for piece in pieces])
    rows = flat.reshape(-1, SIDE * SIDE)
    gathered = lax.all_gather(rows, "chan", axis=0, tiled=False)
    groups = gathered.shape[0]
    gathered = gathered.reshape(groups, -1)
    parts = []
    offset = 0
    for piece in pieces:
        size = piece.size
        part = gathered[:, offset : offset + size]
        parts.append(part.reshape((groups * piece.shape[0],) + piece.shape[1:]))
        offset += size
    return parts


def place_matrix(spots, width):
    columns = lax.broadcasted_iota(jnp.int32, (spots.shape[0], width), 1)
    return (columns == spots[:, None]).astype(jnp.bfloat16)


def interior_spots(first, count):
    pixel = jnp.arange(first, first + count, dtype=jnp.int32)
    return (pixel // SIDE + 1) * (SIDE + 2) + pixel % SIDE + 1


def rim_spots():
    k = jnp.arange(SIDE, dtype=jnp.int32) + 1
    row = SIDE + 2
    return jnp.concatenate([k, k * row + SIDE + 1, (SIDE + 1) * row + k, k * row])


def placed(pieces):
    width = (SIDE + 2) * (SIDE + 2) + 2
    total = None
    for piece, spots in pieces:
        term = jnp.einsum(
            "cbq,qp->cbp", piece, place_matrix(spots, width), preferred_element_type=jnp.float32
        )
        total = term if total is None else total + term
    return total.astype(jnp.bfloat16)


def conv_cm(weight, padded):
    row_width = SIDE + 2
    out_span = SIDE * row_width
    accum = None
    for tap_index in range(9):
        offset = tap_index // 3 * row_width + tap_index % 3
        term = jnp.einsum(
            "oc,cbp->bop",
            weight[tap_index],
            padded[:, :, offset : offset + out_span],
            preferred_element_type=jnp.float32,
        )
        accum = term if accum is None else accum + term
    return accum


def local(
    atmos_state,
    ocean_state,
    atmos_weight,
    ocean_weight,
    couple_weight,
    sea_mask,
    neighbours,
    rotations,
):
    per_dev = atmos_state.shape[0]
    atmos_local = atmos_state.shape[1]
    ocean_local = ocean_state.shape[1]
    groups = lax.axis_size("tiles")
    tile_group = lax.axis_index("tiles")
    first_tile = tile_group * per_dev
    per_owner = per_dev * 3 // 4
    ocean_total = per_owner * groups
    counts = jnp.sum(sea_mask.reshape(groups, per_dev), axis=1)
    starts = jnp.cumsum(counts) - counts
    sea_rank = jnp.cumsum(sea_mask) - 1
    rank_spots = jnp.where(sea_mask == 1, sea_rank, ocean_total)
    tile_of_rank = (
        jnp.zeros((ocean_total,), jnp.int32)
        .at[rank_spots]
        .set(jnp.arange(sea_mask.shape[0], dtype=jnp.int32), mode="drop")
    )
    my_first = starts[tile_group]
    my_last = my_first + counts[tile_group]
    parity = tile_group % 2
    pair_base = tile_group // 2 * 2 * per_owner
    slot_ids = jnp.arange(per_owner, dtype=jnp.int32)
    ranks_send = pair_base + 2 * slot_ids + (1 - parity)
    ranks_own = pair_base + 2 * slot_ids + parity
    send_tile = jnp.clip(tile_of_rank[ranks_send] - first_tile, 0, per_dev - 1)
    own_tile = jnp.clip(tile_of_rank[ranks_own] - first_tile, 0, per_dev - 1)
    from_here = (ranks_own >= my_first) & (ranks_own < my_last)

    own_ocean = jnp.where(
        from_here[:, None, None], ocean_state[own_tile], partner(ocean_state[send_tile], "tiles", 0)
    )

    sea_here = lax.dynamic_slice_in_dim(sea_mask, first_tile, per_dev, 0)
    sea_field = ocean_state * sea_here.astype(jnp.bfloat16)[:, None, None]
    edge_strips = jnp.concatenate([edge_set(atmos_state), edge_set(sea_field)], axis=1)
    widened = padded_2(edge_strips.reshape(per_dev, -1), (("tiles", 0),), per_dev)
    widened = widened.reshape(3 * per_dev, atmos_local + ocean_local, 4, SIDE)
    adjacent = lax.dynamic_slice_in_dim(neighbours, first_tile, per_dev, 0)
    turn_codes = lax.dynamic_slice_in_dim(rotations, first_tile, per_dev, 0)
    local_adjacent = (adjacent // per_dev - tile_group + 1) % groups * per_dev + adjacent % per_dev
    rim_cells = pick_rims(widened, local_adjacent, turn_codes)
    rims_cm = jnp.transpose(rim_cells, (2, 0, 1, 3)).reshape(
        atmos_local + ocean_local, per_dev, 4 * SIDE
    )

    early = 2 * SIDE
    pixels = SIDE * SIDE
    ocean_cm = jnp.transpose(own_ocean, (1, 0, 2))
    atmos_int, atmos_rims, ocean_head = gather_rows(
        [jnp.transpose(atmos_state, (1, 0, 2)), rims_cm[:atmos_local], ocean_cm[:, :, :early]]
    )
    atmos_pad = placed([(atmos_int, interior_spots(0, pixels)), (atmos_rims, rim_spots())])
    atmos_accum = conv_cm(atmos_weight, atmos_pad)
    atmos_next = (
        atmos_state.astype(jnp.float32) + jax.nn.gelu(trim_columns(atmos_accum), approximate=True)
    ).astype(jnp.bfloat16)

    sea_width = ocean_local * 4 * SIDE
    late_block = jnp.concatenate(
        [atmos_next.reshape(per_dev, -1), rim_cells[:, :, atmos_local:].reshape(per_dev, -1)], axis=1
    )
    late_own = jnp.where(
        from_here[:, None], late_block[own_tile], partner(late_block[send_tile], "tiles", 0)
    )
    forcing = late_own[:, : late_block.shape[1] - sea_width].reshape(per_owner, atmos_local, pixels)
    own_rims = late_own[:, late_block.shape[1] - sea_width :].reshape(per_owner, 4, ocean_local, SIDE)
    own_rims = jnp.transpose(own_rims, (2, 0, 1, 3)).reshape(ocean_local, per_owner, 4 * SIDE)

    ocean_tail, ocean_rims, force_all = gather_rows(
        [ocean_cm[:, :, early:], own_rims, jnp.transpose(forcing, (1, 0, 2))]
    )
    ocean_pad = placed(
        [
            (ocean_head, interior_spots(0, early)),
            (ocean_tail, interior_spots(early, pixels - early)),
            (ocean_rims, rim_spots()),
        ]
    )
    conv_accum = conv_cm(ocean_weight, ocean_pad)
    couple_accum = jnp.einsum(
        "oc,cbp->bop", couple_weight, force_all, preferred_element_type=jnp.float32
    )
    mixed = trim_columns(conv_accum) + couple_accum
    ocean_next = (own_ocean.astype(jnp.float32) + jax.nn.gelu(mixed, approximate=True)).astype(
        jnp.bfloat16
    )
    return (atmos_next, ocean_next)


def solution(mesh):
    placed = (
        P("tiles", "chan", None),
        P("tiles", "chan", None),
        P(None, "chan", None),
        P(None, "chan", None),
        P("chan", None),
        P(),
        P(),
        P(),
    )
    return jax.shard_map(
        local,
        mesh=mesh,
        in_specs=placed,
        out_specs=(P("tiles", "chan", None), P("tiles", "chan", None)),
        check_vma=False,
    )
```

```python
import jax
import jax.numpy as jnp
from jax import lax
from jax.sharding import PartitionSpec as P

SIDE = 16


def padded_2(cells, sides, width):
    for axis, dim in sides:
        count = lax.axis_size(axis)
        head = lax.slice_in_dim(cells, 0, width, axis=dim)
        tail = lax.slice_in_dim(cells, cells.shape[dim] - width, cells.shape[dim], axis=dim)
        cells = jnp.concatenate(
            [
                lax.ppermute(tail, axis, [(i, (i + 1) % count) for i in range(count)]),
                cells,
                lax.ppermute(head, axis, [((i + 1) % count, i) for i in range(count)]),
            ],
            axis=dim,
        )
    return cells


def partner(value, axis, distance):
    mask = 2**distance
    pairs = [(source, source ^ mask) for source in range(lax.axis_size(axis))]
    return lax.ppermute(value, axis, pairs)


def edge_set(tile_field):
    tile_count, chan_count = (tile_field.shape[0], tile_field.shape[1])
    tile_grid = tile_field.reshape(tile_count, chan_count, SIDE, SIDE)
    return jnp.stack(
        [
            tile_grid[:, :, 0, :],
            tile_grid[:, :, :, SIDE - 1],
            tile_grid[:, :, SIDE - 1, :],
            tile_grid[:, :, :, 0],
        ],
        axis=2,
    )


def pick_rims(edge_strips, adjacent, turn_codes):
    picked = edge_strips[adjacent]
    side_index = turn_codes % 4
    chosen = picked[:, :, :, 0, :]
    for edge_id in range(1, 4):
        chosen = jnp.where(
            (side_index == edge_id)[:, :, None, None], picked[:, :, :, edge_id, :], chosen
        )
    return jnp.where((turn_codes >= 4)[:, :, None, None], chosen[..., ::-1], chosen)


def pad_tile(tile_field, rim_cells):
    tile_count, chan_count = (tile_field.shape[0], tile_field.shape[1])
    tile_grid = tile_field.reshape(tile_count, chan_count, SIDE, SIDE)
    upper_row = jnp.pad(rim_cells[:, 0], ((0, 0), (0, 0), (1, 1)))[:, :, None, :]
    bottom = jnp.pad(rim_cells[:, 2], ((0, 0), (0, 0), (1, 1)))[:, :, None, :]
    middle = jnp.concatenate(
        [rim_cells[:, 3][:, :, :, None], tile_grid, rim_cells[:, 1][:, :, :, None]], axis=3
    )
    assembled = jnp.concatenate([upper_row, middle, bottom], axis=2).reshape(
        tile_count, chan_count, (SIDE + 2) * (SIDE + 2)
    )
    return jnp.pad(assembled, ((0, 0), (0, 0), (0, 2)))


def trim_columns(accum):
    tile_count, chan_count = (accum.shape[0], accum.shape[1])
    return accum.reshape(tile_count, chan_count, SIDE, SIDE + 2)[:, :, :, :SIDE].reshape(
        tile_count, chan_count, SIDE * SIDE
    )


def conv_step(weight, accum, piece):
    row_width = SIDE + 2
    out_span = SIDE * row_width
    for tap_index in range(9):
        offset = tap_index // 3 * row_width + tap_index % 3
        accum = accum + jnp.einsum(
            "oc,bcp->bop",
            weight[tap_index],
            piece[:, :, offset : offset + out_span],
            preferred_element_type=jnp.float32,
        )
    return accum


def gather_rows(pieces):
    flat = jnp.concatenate([piece.reshape(-1) for piece in pieces])
    rows = flat.reshape(-1, SIDE * SIDE)
    gathered = lax.all_gather(rows, "chan", axis=0, tiled=False)
    groups = gathered.shape[0]
    gathered = gathered.reshape(groups, -1)
    parts = []
    offset = 0
    for piece in pieces:
        size = piece.size
        part = gathered[:, offset : offset + size]
        parts.append(part.reshape((groups * piece.shape[0],) + piece.shape[1:]))
        offset += size
    return parts


def place_matrix(spots, width):
    columns = lax.broadcasted_iota(jnp.int32, (spots.shape[0], width), 1)
    return (columns == spots[:, None]).astype(jnp.bfloat16)


def interior_spots(first, count):
    pixel = jnp.arange(first, first + count, dtype=jnp.int32)
    return (pixel // SIDE + 1) * (SIDE + 2) + pixel % SIDE + 1


def rim_spots():
    k = jnp.arange(SIDE, dtype=jnp.int32) + 1
    row = SIDE + 2
    return jnp.concatenate([k, k * row + SIDE + 1, (SIDE + 1) * row + k, k * row])


def placed(pieces):
    width = (SIDE + 2) * (SIDE + 2) + 2
    total = None
    for piece, spots in pieces:
        term = jnp.einsum(
            "cbq,qp->cbp", piece, place_matrix(spots, width), preferred_element_type=jnp.float32
        )
        total = term if total is None else total + term
    return total.astype(jnp.bfloat16)


def conv_cm(weight, padded):
    row_width = SIDE + 2
    out_span = SIDE * row_width
    taps, out_chans, in_chans = weight.shape
    products = jnp.einsum(
        "kc,cbp->kbp",
        weight.reshape(taps * out_chans, in_chans),
        padded,
        preferred_element_type=jnp.float32,
    ).reshape(taps, out_chans, padded.shape[1], padded.shape[2])
    accum = None
    for tap_index in range(taps):
        offset = tap_index // 3 * row_width + tap_index % 3
        term = products[tap_index, :, :, offset : offset + out_span]
        accum = term if accum is None else accum + term
    return jnp.transpose(accum, (1, 0, 2))


def local(
    atmos_state,
    ocean_state,
    atmos_weight,
    ocean_weight,
    couple_weight,
    sea_mask,
    neighbours,
    rotations,
):
    per_dev = atmos_state.shape[0]
    atmos_local = atmos_state.shape[1]
    ocean_local = ocean_state.shape[1]
    groups = lax.axis_size("tiles")
    tile_group = lax.axis_index("tiles")
    first_tile = tile_group * per_dev
    per_owner = per_dev * 3 // 4
    ocean_total = per_owner * groups
    sea_count = jnp.cumsum(sea_mask)
    parity = tile_group % 2
    pair_base = tile_group // 2 * 2 * per_owner
    slot_ids = jnp.arange(per_owner, dtype=jnp.int32)
    ranks = jnp.concatenate(
        [pair_base + 2 * slot_ids + (1 - parity), pair_base + 2 * slot_ids + parity]
    )
    tiles_of = jnp.sum((sea_count[None, :] <= ranks[:, None]).astype(jnp.int32), axis=1)
    send_tile = jnp.clip(tiles_of[:per_owner] - first_tile, 0, per_dev - 1)
    own_tile = jnp.clip(tiles_of[per_owner:] - first_tile, 0, per_dev - 1)
    from_here = tiles_of[per_owner:] // per_dev == tile_group

    sea_here = lax.dynamic_slice_in_dim(sea_mask, first_tile, per_dev, 0)
    sea_field = ocean_state * sea_here.astype(jnp.bfloat16)[:, None, None]
    edge_strips = jnp.concatenate([edge_set(atmos_state), edge_set(sea_field)], axis=1)
    edge_flat = edge_strips.reshape(-1)
    outgoing = jnp.concatenate([edge_flat, ocean_state[send_tile].reshape(-1)])
    from_left = lax.ppermute(outgoing, "tiles", [(i, (i + 1) % groups) for i in range(groups)])
    from_right = lax.ppermute(outgoing, "tiles", [((i + 1) % groups, i) for i in range(groups)])
    edge_size = edge_flat.shape[0]
    partner_ocean = jnp.where(parity == 0, from_right[edge_size:], from_left[edge_size:])
    own_ocean = jnp.where(
        from_here[:, None, None],
        ocean_state[own_tile],
        partner_ocean.reshape((per_owner,) + ocean_state.shape[1:]),
    )
    widened = jnp.concatenate(
        [from_left[:edge_size], edge_flat, from_right[:edge_size]]
    )
    widened = widened.reshape(3 * per_dev, atmos_local + ocean_local, 4, SIDE)
    adjacent = lax.dynamic_slice_in_dim(neighbours, first_tile, per_dev, 0)
    turn_codes = lax.dynamic_slice_in_dim(rotations, first_tile, per_dev, 0)
    local_adjacent = (adjacent // per_dev - tile_group + 1) % groups * per_dev + adjacent % per_dev
    rim_cells = pick_rims(widened, local_adjacent, turn_codes)
    rims_cm = jnp.transpose(rim_cells, (2, 0, 1, 3)).reshape(
        atmos_local + ocean_local, per_dev, 4 * SIDE
    )

    early = 2 * SIDE
    pixels = SIDE * SIDE
    ocean_cm = jnp.transpose(own_ocean, (1, 0, 2))
    atmos_int, atmos_rims, ocean_head = gather_rows(
        [jnp.transpose(atmos_state, (1, 0, 2)), rims_cm[:atmos_local], ocean_cm[:, :, :early]]
    )
    atmos_pad = placed([(atmos_int, interior_spots(0, pixels)), (atmos_rims, rim_spots())])
    atmos_accum = conv_cm(atmos_weight, atmos_pad)
    atmos_next = (
        atmos_state.astype(jnp.float32) + jax.nn.gelu(trim_columns(atmos_accum), approximate=True)
    ).astype(jnp.bfloat16)

    sea_width = ocean_local * 4 * SIDE
    late_block = jnp.concatenate(
        [atmos_next.reshape(per_dev, -1), rim_cells[:, :, atmos_local:].reshape(per_dev, -1)], axis=1
    )
    late_own = jnp.where(
        from_here[:, None], late_block[own_tile], partner(late_block[send_tile], "tiles", 0)
    )
    forcing = late_own[:, : late_block.shape[1] - sea_width].reshape(per_owner, atmos_local, pixels)
    own_rims = late_own[:, late_block.shape[1] - sea_width :].reshape(per_owner, 4, ocean_local, SIDE)
    own_rims = jnp.transpose(own_rims, (2, 0, 1, 3)).reshape(ocean_local, per_owner, 4 * SIDE)

    ocean_tail, ocean_rims, force_all = gather_rows(
        [ocean_cm[:, :, early:], own_rims, jnp.transpose(forcing, (1, 0, 2))]
    )
    ocean_pad = placed(
        [
            (ocean_head, interior_spots(0, early)),
            (ocean_tail, interior_spots(early, pixels - early)),
            (ocean_rims, rim_spots()),
        ]
    )
    conv_accum = conv_cm(ocean_weight, ocean_pad)
    couple_accum = jnp.einsum(
        "oc,cbp->bop", couple_weight, force_all, preferred_element_type=jnp.float32
    )
    mixed = trim_columns(conv_accum) + couple_accum
    ocean_next = (own_ocean.astype(jnp.float32) + jax.nn.gelu(mixed, approximate=True)).astype(
        jnp.bfloat16
    )
    return (atmos_next, ocean_next)


def solution(mesh):
    placed = (
        P("tiles", "chan", None),
        P("tiles", "chan", None),
        P(None, "chan", None),
        P(None, "chan", None),
        P("chan", None),
        P(),
        P(),
        P(),
    )
    return jax.shard_map(
        local,
        mesh=mesh,
        in_specs=placed,
        out_specs=(P("tiles", "chan", None), P("tiles", "chan", None)),
        check_vma=False,
    )
```

```python
import jax
import jax.numpy as jnp
from jax import lax
from jax.sharding import PartitionSpec as P

SIDE = 16


def padded_2(cells, sides, width):
    for axis, dim in sides:
        count = lax.axis_size(axis)
        head = lax.slice_in_dim(cells, 0, width, axis=dim)
        tail = lax.slice_in_dim(cells, cells.shape[dim] - width, cells.shape[dim], axis=dim)
        cells = jnp.concatenate(
            [
                lax.ppermute(tail, axis, [(i, (i + 1) % count) for i in range(count)]),
                cells,
                lax.ppermute(head, axis, [((i + 1) % count, i) for i in range(count)]),
            ],
            axis=dim,
        )
    return cells


def partner(value, axis, distance):
    mask = 2**distance
    pairs = [(source, source ^ mask) for source in range(lax.axis_size(axis))]
    return lax.ppermute(value, axis, pairs)


def edge_set(tile_field):
    tile_count, chan_count = (tile_field.shape[0], tile_field.shape[1])
    tile_grid = tile_field.reshape(tile_count, chan_count, SIDE, SIDE)
    return jnp.stack(
        [
            tile_grid[:, :, 0, :],
            tile_grid[:, :, :, SIDE - 1],
            tile_grid[:, :, SIDE - 1, :],
            tile_grid[:, :, :, 0],
        ],
        axis=2,
    )


def pick_rims(edge_strips, adjacent, turn_codes):
    picked = edge_strips[adjacent]
    side_index = turn_codes % 4
    chosen = picked[:, :, :, 0, :]
    for edge_id in range(1, 4):
        chosen = jnp.where(
            (side_index == edge_id)[:, :, None, None], picked[:, :, :, edge_id, :], chosen
        )
    return jnp.where((turn_codes >= 4)[:, :, None, None], chosen[..., ::-1], chosen)


def pad_tile(tile_field, rim_cells):
    tile_count, chan_count = (tile_field.shape[0], tile_field.shape[1])
    tile_grid = tile_field.reshape(tile_count, chan_count, SIDE, SIDE)
    upper_row = jnp.pad(rim_cells[:, 0], ((0, 0), (0, 0), (1, 1)))[:, :, None, :]
    bottom = jnp.pad(rim_cells[:, 2], ((0, 0), (0, 0), (1, 1)))[:, :, None, :]
    middle = jnp.concatenate(
        [rim_cells[:, 3][:, :, :, None], tile_grid, rim_cells[:, 1][:, :, :, None]], axis=3
    )
    assembled = jnp.concatenate([upper_row, middle, bottom], axis=2).reshape(
        tile_count, chan_count, (SIDE + 2) * (SIDE + 2)
    )
    return jnp.pad(assembled, ((0, 0), (0, 0), (0, 2)))


def trim_columns(accum):
    tile_count, chan_count = (accum.shape[0], accum.shape[1])
    return accum.reshape(tile_count, chan_count, SIDE, SIDE + 2)[:, :, :, :SIDE].reshape(
        tile_count, chan_count, SIDE * SIDE
    )


def conv_step(weight, accum, piece):
    row_width = SIDE + 2
    out_span = SIDE * row_width
    for tap_index in range(9):
        offset = tap_index // 3 * row_width + tap_index % 3
        accum = accum + jnp.einsum(
            "oc,bcp->bop",
            weight[tap_index],
            piece[:, :, offset : offset + out_span],
            preferred_element_type=jnp.float32,
        )
    return accum


def gather_rows(pieces):
    flat = jnp.concatenate([piece.reshape(-1) for piece in pieces])
    rows = flat.reshape(-1, SIDE * SIDE)
    gathered = lax.all_gather(rows, "chan", axis=0, tiled=False)
    groups = gathered.shape[0]
    gathered = gathered.reshape(groups, -1)
    parts = []
    offset = 0
    for piece in pieces:
        size = piece.size
        part = gathered[:, offset : offset + size]
        parts.append(part.reshape((groups * piece.shape[0],) + piece.shape[1:]))
        offset += size
    return parts


def place_matrix(spots, width):
    columns = lax.broadcasted_iota(jnp.int32, (spots.shape[0], width), 1)
    return (columns == spots[:, None]).astype(jnp.bfloat16)


def interior_spots(first, count):
    pixel = jnp.arange(first, first + count, dtype=jnp.int32)
    return (pixel // SIDE + 1) * (SIDE + 2) + pixel % SIDE + 1


def rim_spots():
    k = jnp.arange(SIDE, dtype=jnp.int32) + 1
    row = SIDE + 2
    return jnp.concatenate([k, k * row + SIDE + 1, (SIDE + 1) * row + k, k * row])


def placed(pieces):
    width = (SIDE + 2) * (SIDE + 2) + 2
    total = None
    for piece, spots in pieces:
        term = jnp.einsum(
            "cbq,qp->bcp", piece, place_matrix(spots, width), preferred_element_type=jnp.float32
        )
        total = term if total is None else total + term
    return total.astype(jnp.bfloat16)


def conv_cm(weight, padded):
    row_width = SIDE + 2
    out_span = SIDE * row_width
    taps, out_chans, in_chans = weight.shape
    tile_count = padded.shape[0]
    products = jnp.einsum(
        "kc,bcp->bkp",
        weight.reshape(taps * out_chans, in_chans),
        padded,
        preferred_element_type=jnp.float32,
    ).reshape(tile_count, taps, out_chans, padded.shape[2])
    accum = None
    for tap_index in range(taps):
        offset = tap_index // 3 * row_width + tap_index % 3
        term = products[:, tap_index, :, offset : offset + out_span]
        accum = term if accum is None else accum + term
    return accum


def pick(selector, values, spec):
    return jnp.einsum(spec, selector, values, preferred_element_type=jnp.float32).astype(
        jnp.bfloat16
    )


def edge_matrix():
    k = jnp.arange(SIDE, dtype=jnp.int32)
    spots = jnp.concatenate([k, k * SIDE + SIDE - 1, (SIDE - 1) * SIDE + k, k * SIDE])
    rows = lax.broadcasted_iota(jnp.int32, (SIDE * SIDE, 4 * SIDE), 0)
    return (rows == spots[None, :]).astype(jnp.bfloat16)


def pair_order(own, other, parity):
    even = jnp.where(parity == 0, own, other)
    odd = jnp.where(parity == 0, other, own)
    return jnp.concatenate([even, odd], axis=0)


def local(
    atmos_state,
    ocean_state,
    atmos_weight,
    ocean_weight,
    couple_weight,
    sea_mask,
    neighbours,
    rotations,
):
    per_dev = atmos_state.shape[0]
    atmos_local = atmos_state.shape[1]
    ocean_local = ocean_state.shape[1]
    chans = atmos_local + ocean_local
    pixels = SIDE * SIDE
    groups = lax.axis_size("tiles")
    tile_group = lax.axis_index("tiles")
    first_tile = tile_group * per_dev
    per_owner = per_dev * 3 // 4
    parity = tile_group % 2

    both_states = jnp.concatenate([atmos_state, ocean_state], axis=1)
    edges_cm = pick(edge_matrix(), both_states, "qe,bcq->cbe")
    sea_here = lax.dynamic_slice_in_dim(sea_mask, first_tile, per_dev, 0).astype(jnp.bfloat16)
    edges_cm = jnp.concatenate(
        [edges_cm[:atmos_local], edges_cm[atmos_local:] * sea_here[None, :, None]], axis=0
    )
    edge_flat = edges_cm.reshape(-1)
    edge_size = edge_flat.shape[0]
    outgoing = jnp.concatenate([edge_flat, ocean_state.reshape(-1)])
    from_left = lax.ppermute(outgoing, "tiles", [(i, (i + 1) % groups) for i in range(groups)])
    from_right = lax.ppermute(outgoing, "tiles", [((i + 1) % groups, i) for i in range(groups)])

    sea_count = jnp.cumsum(sea_mask)
    pair_base = tile_group // 2 * 2 * per_owner
    ranks_own = pair_base + 2 * jnp.arange(per_owner, dtype=jnp.int32) + parity
    tiles_own = jnp.sum((sea_count[None, :] <= ranks_own[:, None]).astype(jnp.int32), axis=1)
    pair_index = tiles_own - tile_group // 2 * 2 * per_dev
    own_pick = (
        pair_index[:, None] == jnp.arange(2 * per_dev, dtype=jnp.int32)[None, :]
    ).astype(jnp.bfloat16)

    adjacent = lax.dynamic_slice_in_dim(neighbours, first_tile, per_dev, 0)
    turn_codes = lax.dynamic_slice_in_dim(rotations, first_tile, per_dev, 0)
    local_adjacent = (adjacent // per_dev - tile_group + 1) % groups * per_dev + adjacent % per_dev
    tile_hit = local_adjacent[None, None, :, :] == jnp.arange(3 * per_dev, dtype=jnp.int32)[
        :, None, None, None
    ]
    edge_hit = (turn_codes % 4)[None, None, :, :] == jnp.arange(4, dtype=jnp.int32)[
        None, :, None, None
    ]
    rim_pick = (tile_hit & edge_hit).astype(jnp.bfloat16).reshape(3 * per_dev * 4, per_dev * 4)
    flip = (
        lax.broadcasted_iota(jnp.int32, (SIDE, SIDE), 0)
        == SIDE - 1 - lax.broadcasted_iota(jnp.int32, (SIDE, SIDE), 1)
    ).astype(jnp.bfloat16)

    partner_state = jnp.where(parity == 0, from_right[edge_size:], from_left[edge_size:])
    pair_state = pair_order(ocean_state, partner_state.reshape(ocean_state.shape), parity)
    ocean_cm = pick(own_pick, pair_state, "st,tcp->csp")
    own_ocean = pick(own_pick, pair_state, "st,tcp->scp")

    widened = jnp.concatenate(
        [
            from_left[:edge_size].reshape(edges_cm.shape),
            edges_cm,
            from_right[:edge_size].reshape(edges_cm.shape),
        ],
        axis=1,
    ).reshape(chans, 3 * per_dev * 4, SIDE)
    straight = pick(rim_pick, widened, "xy,cxk->cyk")
    turned = pick(flip, straight, "kj,cyk->cyj")
    reverse = (turn_codes >= 4).reshape(-1)
    rims_cm = jnp.where(reverse[None, :, None], turned, straight).reshape(chans, per_dev, 4 * SIDE)

    early = 2 * SIDE
    atmos_int, atmos_rims, ocean_head = gather_rows(
        [jnp.transpose(atmos_state, (1, 0, 2)), rims_cm[:atmos_local], ocean_cm[:, :, :early]]
    )
    atmos_pad = placed([(atmos_int, interior_spots(0, pixels)), (atmos_rims, rim_spots())])
    atmos_accum = conv_cm(atmos_weight, atmos_pad)
    atmos_next = (
        atmos_state.astype(jnp.float32) + jax.nn.gelu(trim_columns(atmos_accum), approximate=True)
    ).astype(jnp.bfloat16)

    sea_rims = jnp.transpose(rims_cm[atmos_local:], (1, 0, 2))
    late_block = jnp.concatenate(
        [atmos_next.reshape(per_dev, -1), sea_rims.reshape(per_dev, -1)], axis=1
    )
    pair_late = pair_order(late_block, partner(late_block, "tiles", 0), parity)
    force_width = atmos_local * pixels
    forcing_cm = pick(
        own_pick, pair_late[:, :force_width].reshape(2 * per_dev, atmos_local, pixels), "st,tcp->csp"
    )
    own_rims_cm = pick(
        own_pick, pair_late[:, force_width:].reshape(2 * per_dev, ocean_local, 4 * SIDE), "st,tcp->csp"
    )

    ocean_tail, ocean_rims, force_all = gather_rows(
        [ocean_cm[:, :, early:], own_rims_cm, forcing_cm]
    )
    ocean_pad = placed(
        [
            (ocean_head, interior_spots(0, early)),
            (ocean_tail, interior_spots(early, pixels - early)),
            (ocean_rims, rim_spots()),
        ]
    )
    conv_accum = conv_cm(ocean_weight, ocean_pad)
    couple_accum = jnp.einsum(
        "oc,cbp->bop", couple_weight, force_all, preferred_element_type=jnp.float32
    )
    mixed = trim_columns(conv_accum) + couple_accum
    ocean_next = (own_ocean.astype(jnp.float32) + jax.nn.gelu(mixed, approximate=True)).astype(
        jnp.bfloat16
    )
    return (atmos_next, ocean_next)


def solution(mesh):
    placed = (
        P("tiles", "chan", None),
        P("tiles", "chan", None),
        P(None, "chan", None),
        P(None, "chan", None),
        P("chan", None),
        P(),
        P(),
        P(),
    )
    return jax.shard_map(
        local,
        mesh=mesh,
        in_specs=placed,
        out_specs=(P("tiles", "chan", None), P("tiles", "chan", None)),
        check_vma=False,
    )
```

```python
import jax
import jax.numpy as jnp
from jax import lax
from jax.sharding import PartitionSpec as P

SIDE = 16


def padded_2(cells, sides, width):
    for axis, dim in sides:
        count = lax.axis_size(axis)
        head = lax.slice_in_dim(cells, 0, width, axis=dim)
        tail = lax.slice_in_dim(cells, cells.shape[dim] - width, cells.shape[dim], axis=dim)
        cells = jnp.concatenate(
            [
                lax.ppermute(tail, axis, [(i, (i + 1) % count) for i in range(count)]),
                cells,
                lax.ppermute(head, axis, [((i + 1) % count, i) for i in range(count)]),
            ],
            axis=dim,
        )
    return cells


def partner(value, axis, distance):
    mask = 2**distance
    pairs = [(source, source ^ mask) for source in range(lax.axis_size(axis))]
    return lax.ppermute(value, axis, pairs)


def edge_set(tile_field):
    tile_count, chan_count = (tile_field.shape[0], tile_field.shape[1])
    tile_grid = tile_field.reshape(tile_count, chan_count, SIDE, SIDE)
    return jnp.stack(
        [
            tile_grid[:, :, 0, :],
            tile_grid[:, :, :, SIDE - 1],
            tile_grid[:, :, SIDE - 1, :],
            tile_grid[:, :, :, 0],
        ],
        axis=2,
    )


def pick_rims(edge_strips, adjacent, turn_codes):
    picked = edge_strips[adjacent]
    side_index = turn_codes % 4
    chosen = picked[:, :, :, 0, :]
    for edge_id in range(1, 4):
        chosen = jnp.where(
            (side_index == edge_id)[:, :, None, None], picked[:, :, :, edge_id, :], chosen
        )
    return jnp.where((turn_codes >= 4)[:, :, None, None], chosen[..., ::-1], chosen)


def pad_tile(tile_field, rim_cells):
    tile_count, chan_count = (tile_field.shape[0], tile_field.shape[1])
    tile_grid = tile_field.reshape(tile_count, chan_count, SIDE, SIDE)
    upper_row = jnp.pad(rim_cells[:, 0], ((0, 0), (0, 0), (1, 1)))[:, :, None, :]
    bottom = jnp.pad(rim_cells[:, 2], ((0, 0), (0, 0), (1, 1)))[:, :, None, :]
    middle = jnp.concatenate(
        [rim_cells[:, 3][:, :, :, None], tile_grid, rim_cells[:, 1][:, :, :, None]], axis=3
    )
    assembled = jnp.concatenate([upper_row, middle, bottom], axis=2).reshape(
        tile_count, chan_count, (SIDE + 2) * (SIDE + 2)
    )
    return jnp.pad(assembled, ((0, 0), (0, 0), (0, 2)))


def trim_columns(accum):
    tile_count, chan_count = (accum.shape[0], accum.shape[1])
    return accum.reshape(tile_count, chan_count, SIDE, SIDE + 2)[:, :, :, :SIDE].reshape(
        tile_count, chan_count, SIDE * SIDE
    )


def conv_step(weight, accum, piece):
    row_width = SIDE + 2
    out_span = SIDE * row_width
    for tap_index in range(9):
        offset = tap_index // 3 * row_width + tap_index % 3
        accum = accum + jnp.einsum(
            "oc,bcp->bop",
            weight[tap_index],
            piece[:, :, offset : offset + out_span],
            preferred_element_type=jnp.float32,
        )
    return accum


def gather_rows(pieces):
    flat = jnp.concatenate([piece.reshape(-1) for piece in pieces])
    rows = flat.reshape(-1, SIDE * SIDE)
    gathered = lax.all_gather(rows, "chan", axis=0, tiled=False)
    groups = gathered.shape[0]
    gathered = gathered.reshape(groups, -1)
    parts = []
    offset = 0
    for piece in pieces:
        size = piece.size
        part = gathered[:, offset : offset + size]
        parts.append(part.reshape((groups * piece.shape[0],) + piece.shape[1:]))
        offset += size
    return parts


def place_matrix(spots, width):
    columns = lax.broadcasted_iota(jnp.int32, (spots.shape[0], width), 1)
    return (columns == spots[:, None]).astype(jnp.bfloat16)


def interior_spots(first, count):
    pixel = jnp.arange(first, first + count, dtype=jnp.int32)
    return (pixel // SIDE + 1) * (SIDE + 2) + pixel % SIDE + 1


def rim_spots():
    k = jnp.arange(SIDE, dtype=jnp.int32) + 1
    row = SIDE + 2
    return jnp.concatenate([k, k * row + SIDE + 1, (SIDE + 1) * row + k, k * row])


def placed(pieces):
    width = (SIDE + 2) * (SIDE + 2) + 2
    total = None
    for piece, spots in pieces:
        term = jnp.einsum(
            "cbq,qp->cbp", piece, place_matrix(spots, width), preferred_element_type=jnp.float32
        )
        total = term if total is None else total + term
    return total.astype(jnp.bfloat16)


def conv_cm(weight, padded):
    row_width = SIDE + 2
    out_span = SIDE * row_width
    products = jnp.einsum("toc,cbp->tobp", weight, padded, preferred_element_type=jnp.float32)
    accum = None
    for tap_index in range(weight.shape[0]):
        offset = tap_index // 3 * row_width + tap_index % 3
        term = products[tap_index, :, :, offset : offset + out_span]
        accum = term if accum is None else accum + term
    return jnp.transpose(accum, (1, 0, 2))


def pick(selector, values, spec):
    return jnp.einsum(spec, selector, values, preferred_element_type=jnp.float32).astype(
        jnp.bfloat16
    )


def edge_matrix():
    k = jnp.arange(SIDE, dtype=jnp.int32)
    spots = jnp.concatenate([k, k * SIDE + SIDE - 1, (SIDE - 1) * SIDE + k, k * SIDE])
    rows = lax.broadcasted_iota(jnp.int32, (SIDE * SIDE, 4 * SIDE), 0)
    return (rows == spots[None, :]).astype(jnp.bfloat16)


def pair_order(own, other, parity):
    even = jnp.where(parity == 0, own, other)
    odd = jnp.where(parity == 0, other, own)
    return jnp.concatenate([even, odd], axis=0)


def local(
    atmos_state,
    ocean_state,
    atmos_weight,
    ocean_weight,
    couple_weight,
    sea_mask,
    neighbours,
    rotations,
):
    per_dev = atmos_state.shape[0]
    atmos_local = atmos_state.shape[1]
    ocean_local = ocean_state.shape[1]
    chans = atmos_local + ocean_local
    pixels = SIDE * SIDE
    groups = lax.axis_size("tiles")
    tile_group = lax.axis_index("tiles")
    first_tile = tile_group * per_dev
    per_owner = per_dev * 3 // 4
    parity = tile_group % 2

    both_states = jnp.concatenate([atmos_state, ocean_state], axis=1)
    edges_cm = pick(edge_matrix(), both_states, "qe,bcq->cbe")
    tables = lax.dynamic_slice_in_dim(
        jnp.concatenate([neighbours, rotations, sea_mask[:, None]], axis=1), first_tile, per_dev, 0
    )
    sea_here = tables[:, 8].astype(jnp.bfloat16)
    edges_cm = jnp.concatenate(
        [edges_cm[:atmos_local], edges_cm[atmos_local:] * sea_here[None, :, None]], axis=0
    )
    edge_flat = edges_cm.reshape(-1)
    edge_size = edge_flat.shape[0]
    outgoing = jnp.concatenate([edge_flat, ocean_state.reshape(-1)])
    from_left = lax.ppermute(outgoing, "tiles", [(i, (i + 1) % groups) for i in range(groups)])
    from_right = lax.ppermute(outgoing, "tiles", [((i + 1) % groups, i) for i in range(groups)])

    pair_tiles = 2 * per_dev
    pair_first = tile_group // 2 * pair_tiles
    pair_mask = lax.dynamic_slice_in_dim(sea_mask, pair_first, pair_tiles, 0)
    upto = (
        lax.broadcasted_iota(jnp.int32, (pair_tiles, pair_tiles), 1)
        <= lax.broadcasted_iota(jnp.int32, (pair_tiles, pair_tiles), 0)
    )
    pair_count = jnp.sum(jnp.where(upto, pair_mask[None, :], 0), axis=1)
    local_rank = 2 * jnp.arange(per_owner, dtype=jnp.int32) + parity
    pair_index = jnp.sum((pair_count[None, :] <= local_rank[:, None]).astype(jnp.int32), axis=1)
    own_pick = (
        pair_index[:, None] == jnp.arange(pair_tiles, dtype=jnp.int32)[None, :]
    ).astype(jnp.bfloat16)

    adjacent = tables[:, :4]
    turn_codes = tables[:, 4:8]
    local_adjacent = (adjacent // per_dev - tile_group + 1) % groups * per_dev + adjacent % per_dev
    tile_hit = local_adjacent[None, None, :, :] == jnp.arange(3 * per_dev, dtype=jnp.int32)[
        :, None, None, None
    ]
    edge_hit = (turn_codes % 4)[None, None, :, :] == jnp.arange(4, dtype=jnp.int32)[
        None, :, None, None
    ]
    rim_pick = (tile_hit & edge_hit).astype(jnp.bfloat16).reshape(3 * per_dev * 4, per_dev * 4)
    flip = (
        lax.broadcasted_iota(jnp.int32, (SIDE, SIDE), 0)
        == SIDE - 1 - lax.broadcasted_iota(jnp.int32, (SIDE, SIDE), 1)
    ).astype(jnp.bfloat16)

    partner_state = jnp.where(parity == 0, from_right[edge_size:], from_left[edge_size:])
    pair_state = pair_order(ocean_state, partner_state.reshape(ocean_state.shape), parity)
    ocean_cm = pick(own_pick, pair_state, "st,tcp->csp")
    own_ocean = pick(own_pick, pair_state, "st,tcp->scp")

    widened = jnp.concatenate(
        [
            from_left[:edge_size].reshape(edges_cm.shape),
            edges_cm,
            from_right[:edge_size].reshape(edges_cm.shape),
        ],
        axis=1,
    ).reshape(chans, 3 * per_dev * 4, SIDE)
    straight = pick(rim_pick, widened, "xy,cxk->cyk")
    turned = pick(flip, straight, "kj,cyk->cyj")
    reverse = (turn_codes >= 4).reshape(-1)
    rims_cm = jnp.where(reverse[None, :, None], turned, straight).reshape(chans, per_dev, 4 * SIDE)

    early = 2 * SIDE
    atmos_int, atmos_rims, ocean_head = gather_rows(
        [jnp.transpose(atmos_state, (1, 0, 2)), rims_cm[:atmos_local], ocean_cm[:, :, :early]]
    )
    atmos_pad = placed([(atmos_int, interior_spots(0, pixels)), (atmos_rims, rim_spots())])
    atmos_accum = conv_cm(atmos_weight, atmos_pad)
    atmos_next = (
        atmos_state.astype(jnp.float32) + jax.nn.gelu(trim_columns(atmos_accum), approximate=True)
    ).astype(jnp.bfloat16)

    sea_rims = jnp.transpose(rims_cm[atmos_local:], (1, 0, 2))
    late_block = jnp.concatenate(
        [atmos_next.reshape(per_dev, -1), sea_rims.reshape(per_dev, -1)], axis=1
    )
    pair_late = pair_order(late_block, partner(late_block, "tiles", 0), parity)
    force_width = atmos_local * pixels
    forcing_cm = pick(
        own_pick, pair_late[:, :force_width].reshape(2 * per_dev, atmos_local, pixels), "st,tcp->csp"
    )
    own_rims_cm = pick(
        own_pick, pair_late[:, force_width:].reshape(2 * per_dev, ocean_local, 4 * SIDE), "st,tcp->csp"
    )

    ocean_tail, ocean_rims, force_all = gather_rows(
        [ocean_cm[:, :, early:], own_rims_cm, forcing_cm]
    )
    ocean_pad = placed(
        [
            (ocean_head, interior_spots(0, early)),
            (ocean_tail, interior_spots(early, pixels - early)),
            (ocean_rims, rim_spots()),
        ]
    )
    conv_accum = conv_cm(ocean_weight, ocean_pad)
    couple_accum = jnp.einsum(
        "oc,cbp->bop", couple_weight, force_all, preferred_element_type=jnp.float32
    )
    mixed = trim_columns(conv_accum) + couple_accum
    ocean_next = (own_ocean.astype(jnp.float32) + jax.nn.gelu(mixed, approximate=True)).astype(
        jnp.bfloat16
    )
    return (atmos_next, ocean_next)


def solution(mesh):
    placed = (
        P("tiles", "chan", None),
        P("tiles", "chan", None),
        P(None, "chan", None),
        P(None, "chan", None),
        P("chan", None),
        P(),
        P(),
        P(),
    )
    return jax.shard_map(
        local,
        mesh=mesh,
        in_specs=placed,
        out_specs=(P("tiles", "chan", None), P("tiles", "chan", None)),
        check_vma=False,
    )
```

```python
import jax
import jax.numpy as jnp
from jax import lax
from jax.sharding import PartitionSpec as P

SIDE = 16


def padded_2(cells, sides, width):
    for axis, dim in sides:
        count = lax.axis_size(axis)
        head = lax.slice_in_dim(cells, 0, width, axis=dim)
        tail = lax.slice_in_dim(cells, cells.shape[dim] - width, cells.shape[dim], axis=dim)
        cells = jnp.concatenate(
            [
                lax.ppermute(tail, axis, [(i, (i + 1) % count) for i in range(count)]),
                cells,
                lax.ppermute(head, axis, [((i + 1) % count, i) for i in range(count)]),
            ],
            axis=dim,
        )
    return cells


def partner(value, axis, distance):
    mask = 2**distance
    pairs = [(source, source ^ mask) for source in range(lax.axis_size(axis))]
    return lax.ppermute(value, axis, pairs)


def edge_set(tile_field):
    tile_count, chan_count = (tile_field.shape[0], tile_field.shape[1])
    tile_grid = tile_field.reshape(tile_count, chan_count, SIDE, SIDE)
    return jnp.stack(
        [
            tile_grid[:, :, 0, :],
            tile_grid[:, :, :, SIDE - 1],
            tile_grid[:, :, SIDE - 1, :],
            tile_grid[:, :, :, 0],
        ],
        axis=2,
    )


def pick_rims(edge_strips, adjacent, turn_codes):
    picked = edge_strips[adjacent]
    side_index = turn_codes % 4
    chosen = picked[:, :, :, 0, :]
    for edge_id in range(1, 4):
        chosen = jnp.where(
            (side_index == edge_id)[:, :, None, None], picked[:, :, :, edge_id, :], chosen
        )
    return jnp.where((turn_codes >= 4)[:, :, None, None], chosen[..., ::-1], chosen)


def pad_tile(tile_field, rim_cells):
    tile_count, chan_count = (tile_field.shape[0], tile_field.shape[1])
    tile_grid = tile_field.reshape(tile_count, chan_count, SIDE, SIDE)
    upper_row = jnp.pad(rim_cells[:, 0], ((0, 0), (0, 0), (1, 1)))[:, :, None, :]
    bottom = jnp.pad(rim_cells[:, 2], ((0, 0), (0, 0), (1, 1)))[:, :, None, :]
    middle = jnp.concatenate(
        [rim_cells[:, 3][:, :, :, None], tile_grid, rim_cells[:, 1][:, :, :, None]], axis=3
    )
    assembled = jnp.concatenate([upper_row, middle, bottom], axis=2).reshape(
        tile_count, chan_count, (SIDE + 2) * (SIDE + 2)
    )
    return jnp.pad(assembled, ((0, 0), (0, 0), (0, 2)))


def trim_columns(accum):
    tile_count, chan_count = (accum.shape[0], accum.shape[1])
    return accum.reshape(tile_count, chan_count, SIDE, SIDE + 2)[:, :, :, :SIDE].reshape(
        tile_count, chan_count, SIDE * SIDE
    )


def conv_step(weight, accum, piece):
    row_width = SIDE + 2
    out_span = SIDE * row_width
    for tap_index in range(9):
        offset = tap_index // 3 * row_width + tap_index % 3
        accum = accum + jnp.einsum(
            "oc,bcp->bop",
            weight[tap_index],
            piece[:, :, offset : offset + out_span],
            preferred_element_type=jnp.float32,
        )
    return accum


def gather_rows(pieces):
    flat = jnp.concatenate([piece.reshape(-1) for piece in pieces])
    rows = flat.reshape(-1, SIDE * SIDE)
    gathered = lax.all_gather(rows, "chan", axis=0, tiled=False)
    groups = gathered.shape[0]
    gathered = gathered.reshape(groups, -1)
    parts = []
    offset = 0
    for piece in pieces:
        size = piece.size
        part = gathered[:, offset : offset + size]
        parts.append(part.reshape((groups * piece.shape[0],) + piece.shape[1:]))
        offset += size
    return parts


def place_matrix(spots, width):
    columns = lax.broadcasted_iota(jnp.int32, (spots.shape[0], width), 1)
    return (columns == spots[:, None]).astype(jnp.bfloat16)


def interior_spots(first, count):
    pixel = jnp.arange(first, first + count, dtype=jnp.int32)
    return (pixel // SIDE + 1) * (SIDE + 2) + pixel % SIDE + 1


def rim_spots():
    k = jnp.arange(SIDE, dtype=jnp.int32) + 1
    row = SIDE + 2
    return jnp.concatenate([k, k * row + SIDE + 1, (SIDE + 1) * row + k, k * row])


def placed(pieces):
    width = (SIDE + 2) * (SIDE + 2) + 2
    total = None
    for piece, spots in pieces:
        term = jnp.einsum(
            "cbq,qp->bcp", piece, place_matrix(spots, width), preferred_element_type=jnp.float32
        )
        total = term if total is None else total + term
    return total.astype(jnp.bfloat16)


def conv_cm(weight, padded):
    row_width = SIDE + 2
    out_span = SIDE * row_width
    taps, out_chans, in_chans = weight.shape
    rows = -(-out_chans // 8) * 8
    weight = jnp.pad(weight, ((0, 0), (0, rows - out_chans), (0, 0)))
    tile_count = padded.shape[0]
    products = jnp.einsum(
        "kc,bcp->bkp",
        weight.reshape(taps * rows, in_chans),
        padded,
        preferred_element_type=jnp.float32,
    ).reshape(tile_count, taps, rows, padded.shape[2])
    accum = None
    for tap_index in range(taps):
        offset = tap_index // 3 * row_width + tap_index % 3
        term = products[:, tap_index, :out_chans, offset : offset + out_span]
        accum = term if accum is None else accum + term
    return accum


def pick(selector, values, spec):
    return jnp.einsum(spec, selector, values, preferred_element_type=jnp.float32).astype(
        jnp.bfloat16
    )


def edge_matrix():
    k = jnp.arange(SIDE, dtype=jnp.int32)
    spots = jnp.concatenate([k, k * SIDE + SIDE - 1, (SIDE - 1) * SIDE + k, k * SIDE])
    rows = lax.broadcasted_iota(jnp.int32, (SIDE * SIDE, 4 * SIDE), 0)
    return (rows == spots[None, :]).astype(jnp.bfloat16)


def pair_order(own, other, parity):
    even = jnp.where(parity == 0, own, other)
    odd = jnp.where(parity == 0, other, own)
    return jnp.concatenate([even, odd], axis=0)


def local(
    atmos_state,
    ocean_state,
    atmos_weight,
    ocean_weight,
    couple_weight,
    sea_mask,
    neighbours,
    rotations,
):
    per_dev = atmos_state.shape[0]
    atmos_local = atmos_state.shape[1]
    ocean_local = ocean_state.shape[1]
    chans = atmos_local + ocean_local
    pixels = SIDE * SIDE
    groups = lax.axis_size("tiles")
    tile_group = lax.axis_index("tiles")
    first_tile = tile_group * per_dev
    per_owner = per_dev * 3 // 4
    parity = tile_group % 2

    both_states = jnp.concatenate([atmos_state, ocean_state], axis=1)
    edges_cm = pick(edge_matrix(), both_states, "qe,bcq->cbe")
    tables = lax.dynamic_slice_in_dim(
        jnp.concatenate([neighbours, rotations, sea_mask[:, None]], axis=1), first_tile, per_dev, 0
    )
    sea_here = tables[:, 8].astype(jnp.bfloat16)
    edges_cm = jnp.concatenate(
        [edges_cm[:atmos_local], edges_cm[atmos_local:] * sea_here[None, :, None]], axis=0
    )
    edge_flat = edges_cm.reshape(-1)
    edge_size = edge_flat.shape[0]
    outgoing = jnp.concatenate([edge_flat, ocean_state.reshape(-1)])
    from_left = lax.ppermute(outgoing, "tiles", [(i, (i + 1) % groups) for i in range(groups)])
    from_right = lax.ppermute(outgoing, "tiles", [((i + 1) % groups, i) for i in range(groups)])

    pair_tiles = 2 * per_dev
    pair_first = tile_group // 2 * pair_tiles
    pair_mask = lax.dynamic_slice_in_dim(sea_mask, pair_first, pair_tiles, 0)
    upto = (
        lax.broadcasted_iota(jnp.int32, (pair_tiles, pair_tiles), 1)
        <= lax.broadcasted_iota(jnp.int32, (pair_tiles, pair_tiles), 0)
    )
    pair_count = jnp.sum(jnp.where(upto, pair_mask[None, :], 0), axis=1)
    local_rank = 2 * jnp.arange(per_owner, dtype=jnp.int32) + parity
    pair_index = jnp.sum((pair_count[None, :] <= local_rank[:, None]).astype(jnp.int32), axis=1)
    own_pick = (
        pair_index[:, None] == jnp.arange(pair_tiles, dtype=jnp.int32)[None, :]
    ).astype(jnp.bfloat16)

    adjacent = tables[:, :4]
    turn_codes = tables[:, 4:8]
    local_adjacent = (adjacent // per_dev - tile_group + 1) % groups * per_dev + adjacent % per_dev
    tile_hit = local_adjacent[None, None, :, :] == jnp.arange(3 * per_dev, dtype=jnp.int32)[
        :, None, None, None
    ]
    edge_hit = (turn_codes % 4)[None, None, :, :] == jnp.arange(4, dtype=jnp.int32)[
        None, :, None, None
    ]
    rim_pick = (tile_hit & edge_hit).astype(jnp.bfloat16).reshape(3 * per_dev * 4, per_dev * 4)
    flip = (
        lax.broadcasted_iota(jnp.int32, (SIDE, SIDE), 0)
        == SIDE - 1 - lax.broadcasted_iota(jnp.int32, (SIDE, SIDE), 1)
    ).astype(jnp.bfloat16)

    partner_state = jnp.where(parity == 0, from_right[edge_size:], from_left[edge_size:])
    pair_state = pair_order(ocean_state, partner_state.reshape(ocean_state.shape), parity)
    ocean_cm = pick(own_pick, pair_state, "st,tcp->csp")
    own_ocean = pick(own_pick, pair_state, "st,tcp->scp")

    widened = jnp.concatenate(
        [
            from_left[:edge_size].reshape(edges_cm.shape),
            edges_cm,
            from_right[:edge_size].reshape(edges_cm.shape),
        ],
        axis=1,
    ).reshape(chans, 3 * per_dev * 4, SIDE)
    straight = pick(rim_pick, widened, "xy,cxk->cyk")
    turned = pick(flip, straight, "kj,cyk->cyj")
    reverse = (turn_codes >= 4).reshape(-1)
    rims_cm = jnp.where(reverse[None, :, None], turned, straight).reshape(chans, per_dev, 4 * SIDE)

    early = 2 * SIDE
    atmos_int, atmos_rims, ocean_head = gather_rows(
        [jnp.transpose(atmos_state, (1, 0, 2)), rims_cm[:atmos_local], ocean_cm[:, :, :early]]
    )
    atmos_pad = placed([(atmos_int, interior_spots(0, pixels)), (atmos_rims, rim_spots())])
    atmos_accum = conv_cm(atmos_weight, atmos_pad)
    atmos_next = (
        atmos_state.astype(jnp.float32) + jax.nn.gelu(trim_columns(atmos_accum), approximate=True)
    ).astype(jnp.bfloat16)

    sea_rims = jnp.transpose(rims_cm[atmos_local:], (1, 0, 2))
    late_block = jnp.concatenate(
        [atmos_next.reshape(per_dev, -1), sea_rims.reshape(per_dev, -1)], axis=1
    )
    pair_late = pair_order(late_block, partner(late_block, "tiles", 0), parity)
    force_width = atmos_local * pixels
    forcing_cm = pick(
        own_pick, pair_late[:, :force_width].reshape(2 * per_dev, atmos_local, pixels), "st,tcp->csp"
    )
    own_rims_cm = pick(
        own_pick, pair_late[:, force_width:].reshape(2 * per_dev, ocean_local, 4 * SIDE), "st,tcp->csp"
    )

    ocean_tail, ocean_rims, force_all = gather_rows(
        [ocean_cm[:, :, early:], own_rims_cm, forcing_cm]
    )
    ocean_pad = placed(
        [
            (ocean_head, interior_spots(0, early)),
            (ocean_tail, interior_spots(early, pixels - early)),
            (ocean_rims, rim_spots()),
        ]
    )
    conv_accum = conv_cm(ocean_weight, ocean_pad)
    couple_accum = jnp.einsum(
        "oc,cbp->bop", couple_weight, force_all, preferred_element_type=jnp.float32
    )
    mixed = trim_columns(conv_accum) + couple_accum
    ocean_next = (own_ocean.astype(jnp.float32) + jax.nn.gelu(mixed, approximate=True)).astype(
        jnp.bfloat16
    )
    return (atmos_next, ocean_next)


def solution(mesh):
    placed = (
        P("tiles", "chan", None),
        P("tiles", "chan", None),
        P(None, "chan", None),
        P(None, "chan", None),
        P("chan", None),
        P(),
        P(),
        P(),
    )
    return jax.shard_map(
        local,
        mesh=mesh,
        in_specs=placed,
        out_specs=(P("tiles", "chan", None), P("tiles", "chan", None)),
        check_vma=False,
    )
```

```python
import jax
import jax.numpy as jnp
from jax import lax
from jax.sharding import PartitionSpec as P

SIDE = 16


def padded_2(cells, sides, width):
    for axis, dim in sides:
        count = lax.axis_size(axis)
        head = lax.slice_in_dim(cells, 0, width, axis=dim)
        tail = lax.slice_in_dim(cells, cells.shape[dim] - width, cells.shape[dim], axis=dim)
        cells = jnp.concatenate(
            [
                lax.ppermute(tail, axis, [(i, (i + 1) % count) for i in range(count)]),
                cells,
                lax.ppermute(head, axis, [((i + 1) % count, i) for i in range(count)]),
            ],
            axis=dim,
        )
    return cells


def partner(value, axis, distance):
    mask = 2**distance
    pairs = [(source, source ^ mask) for source in range(lax.axis_size(axis))]
    return lax.ppermute(value, axis, pairs)


def edge_set(tile_field):
    tile_count, chan_count = (tile_field.shape[0], tile_field.shape[1])
    tile_grid = tile_field.reshape(tile_count, chan_count, SIDE, SIDE)
    return jnp.stack(
        [
            tile_grid[:, :, 0, :],
            tile_grid[:, :, :, SIDE - 1],
            tile_grid[:, :, SIDE - 1, :],
            tile_grid[:, :, :, 0],
        ],
        axis=2,
    )


def pick_rims(edge_strips, adjacent, turn_codes):
    picked = edge_strips[adjacent]
    side_index = turn_codes % 4
    chosen = picked[:, :, :, 0, :]
    for edge_id in range(1, 4):
        chosen = jnp.where(
            (side_index == edge_id)[:, :, None, None], picked[:, :, :, edge_id, :], chosen
        )
    return jnp.where((turn_codes >= 4)[:, :, None, None], chosen[..., ::-1], chosen)


def pad_tile(tile_field, rim_cells):
    tile_count, chan_count = (tile_field.shape[0], tile_field.shape[1])
    tile_grid = tile_field.reshape(tile_count, chan_count, SIDE, SIDE)
    upper_row = jnp.pad(rim_cells[:, 0], ((0, 0), (0, 0), (1, 1)))[:, :, None, :]
    bottom = jnp.pad(rim_cells[:, 2], ((0, 0), (0, 0), (1, 1)))[:, :, None, :]
    middle = jnp.concatenate(
        [rim_cells[:, 3][:, :, :, None], tile_grid, rim_cells[:, 1][:, :, :, None]], axis=3
    )
    assembled = jnp.concatenate([upper_row, middle, bottom], axis=2).reshape(
        tile_count, chan_count, (SIDE + 2) * (SIDE + 2)
    )
    return jnp.pad(assembled, ((0, 0), (0, 0), (0, 2)))


def trim_columns(accum):
    tile_count, chan_count = (accum.shape[0], accum.shape[1])
    return accum.reshape(tile_count, chan_count, SIDE, SIDE + 2)[:, :, :, :SIDE].reshape(
        tile_count, chan_count, SIDE * SIDE
    )


def conv_step(weight, accum, piece):
    row_width = SIDE + 2
    out_span = SIDE * row_width
    for tap_index in range(9):
        offset = tap_index // 3 * row_width + tap_index % 3
        accum = accum + jnp.einsum(
            "oc,bcp->bop",
            weight[tap_index],
            piece[:, :, offset : offset + out_span],
            preferred_element_type=jnp.float32,
        )
    return accum


def gather_rows(pieces):
    flat = jnp.concatenate([piece.reshape(-1) for piece in pieces])
    rows = flat.reshape(-1, SIDE * SIDE)
    gathered = lax.all_gather(rows, "chan", axis=0, tiled=False)
    groups = gathered.shape[0]
    gathered = gathered.reshape(groups, -1)
    parts = []
    offset = 0
    for piece in pieces:
        size = piece.size
        part = gathered[:, offset : offset + size]
        parts.append(part.reshape((groups * piece.shape[0],) + piece.shape[1:]))
        offset += size
    return parts


def place_matrix(spots, width):
    columns = lax.broadcasted_iota(jnp.int32, (spots.shape[0], width), 1)
    return (columns == spots[:, None]).astype(jnp.bfloat16)


def interior_spots(first, count):
    pixel = jnp.arange(first, first + count, dtype=jnp.int32)
    return (pixel // SIDE + 1) * (SIDE + 2) + pixel % SIDE + 1


def rim_spots():
    k = jnp.arange(SIDE, dtype=jnp.int32) + 1
    row = SIDE + 2
    return jnp.concatenate([k, k * row + SIDE + 1, (SIDE + 1) * row + k, k * row])


def placed(pieces):
    width = (SIDE + 2) * (SIDE + 2) + 2
    total = None
    for piece, spots in pieces:
        term = jnp.einsum(
            "cbq,qp->bcp", piece, place_matrix(spots, width), preferred_element_type=jnp.float32
        )
        total = term if total is None else total + term
    return total.astype(jnp.bfloat16)


def conv_cm(weight, padded):
    row_width = SIDE + 2
    out_span = SIDE * row_width
    taps, out_chans, in_chans = weight.shape
    rows = -(-out_chans // 8) * 8
    weight = jnp.pad(weight, ((0, 0), (0, rows - out_chans), (0, 0)))
    tile_count = padded.shape[0]
    products = jnp.einsum(
        "kc,bcp->bkp",
        weight.reshape(taps * rows, in_chans),
        padded,
        preferred_element_type=jnp.float32,
    ).reshape(tile_count, taps, rows, padded.shape[2])
    accum = None
    for tap_index in range(taps):
        offset = tap_index // 3 * row_width + tap_index % 3
        term = products[:, tap_index, :out_chans, offset : offset + out_span]
        accum = term if accum is None else accum + term
    return accum


def pick(selector, values, spec):
    return jnp.einsum(spec, selector, values, preferred_element_type=jnp.float32).astype(
        jnp.bfloat16
    )


def edge_matrix():
    k = jnp.arange(SIDE, dtype=jnp.int32)
    spots = jnp.concatenate([k, k * SIDE + SIDE - 1, (SIDE - 1) * SIDE + k, k * SIDE])
    rows = lax.broadcasted_iota(jnp.int32, (SIDE * SIDE, 4 * SIDE), 0)
    return (rows == spots[None, :]).astype(jnp.bfloat16)


def pair_order(own, other, parity):
    even = jnp.where(parity == 0, own, other)
    odd = jnp.where(parity == 0, other, own)
    return jnp.concatenate([even, odd], axis=0)


def local(
    atmos_state,
    ocean_state,
    atmos_weight,
    ocean_weight,
    couple_weight,
    sea_mask,
    neighbours,
    rotations,
):
    per_dev = atmos_state.shape[0]
    atmos_local = atmos_state.shape[1]
    ocean_local = ocean_state.shape[1]
    chans = atmos_local + ocean_local
    pixels = SIDE * SIDE
    groups = lax.axis_size("tiles")
    tile_group = lax.axis_index("tiles")
    first_tile = tile_group * per_dev
    per_owner = per_dev * 3 // 4
    parity = tile_group % 2

    tables = lax.dynamic_slice_in_dim(
        jnp.concatenate([neighbours, rotations, sea_mask[:, None]], axis=1), first_tile, per_dev, 0
    )
    sea_here = tables[:, 8].astype(jnp.bfloat16)
    edge_pick = edge_matrix()
    edges_cm = jnp.concatenate(
        [
            pick(edge_pick, atmos_state, "qe,bcq->cbe"),
            pick(edge_pick, ocean_state, "qe,bcq->cbe") * sea_here[None, :, None],
        ],
        axis=0,
    )
    edge_rows = edges_cm.size // pixels
    outgoing = jnp.concatenate(
        [edges_cm.reshape(edge_rows, pixels), ocean_state.reshape(-1, pixels)], axis=0
    )
    from_left = lax.ppermute(outgoing, "tiles", [(i, (i + 1) % groups) for i in range(groups)])
    from_right = lax.ppermute(outgoing, "tiles", [((i + 1) % groups, i) for i in range(groups)])

    pair_tiles = 2 * per_dev
    pair_first = tile_group // 2 * pair_tiles
    pair_mask = lax.dynamic_slice_in_dim(sea_mask, pair_first, pair_tiles, 0)
    upto = (
        lax.broadcasted_iota(jnp.int32, (pair_tiles, pair_tiles), 1)
        <= lax.broadcasted_iota(jnp.int32, (pair_tiles, pair_tiles), 0)
    )
    pair_count = jnp.sum(jnp.where(upto, pair_mask[None, :], 0), axis=1)
    local_rank = 2 * jnp.arange(per_owner, dtype=jnp.int32) + parity
    pair_index = jnp.sum((pair_count[None, :] <= local_rank[:, None]).astype(jnp.int32), axis=1)
    own_pick = (
        pair_index[:, None] == jnp.arange(pair_tiles, dtype=jnp.int32)[None, :]
    ).astype(jnp.bfloat16)

    adjacent = tables[:, :4]
    turn_codes = tables[:, 4:8]
    local_adjacent = (adjacent // per_dev - tile_group + 1) % groups * per_dev + adjacent % per_dev
    tile_hit = local_adjacent[None, None, :, :] == jnp.arange(3 * per_dev, dtype=jnp.int32)[
        :, None, None, None
    ]
    edge_hit = (turn_codes % 4)[None, None, :, :] == jnp.arange(4, dtype=jnp.int32)[
        None, :, None, None
    ]
    rim_pick = (tile_hit & edge_hit).astype(jnp.bfloat16).reshape(3 * per_dev * 4, per_dev * 4)
    flip = (
        lax.broadcasted_iota(jnp.int32, (SIDE, SIDE), 0)
        == SIDE - 1 - lax.broadcasted_iota(jnp.int32, (SIDE, SIDE), 1)
    ).astype(jnp.bfloat16)

    partner_state = jnp.where(parity == 0, from_right[edge_rows:], from_left[edge_rows:])
    pair_state = pair_order(ocean_state, partner_state.reshape(ocean_state.shape), parity)
    ocean_cm = pick(own_pick, pair_state, "st,tcp->csp")
    own_ocean = pick(own_pick, pair_state, "st,tcp->scp")

    widened = jnp.concatenate(
        [
            from_left[:edge_rows].reshape(edges_cm.shape),
            edges_cm,
            from_right[:edge_rows].reshape(edges_cm.shape),
        ],
        axis=1,
    ).reshape(chans, 3 * per_dev * 4, SIDE)
    straight = pick(rim_pick, widened, "xy,cxk->cyk")
    turned = pick(flip, straight, "kj,cyk->cyj")
    reverse = (turn_codes >= 4).reshape(-1)
    rims_cm = jnp.where(reverse[None, :, None], turned, straight).reshape(chans, per_dev, 4 * SIDE)

    early = 2 * SIDE
    atmos_int, atmos_rims, ocean_head = gather_rows(
        [jnp.transpose(atmos_state, (1, 0, 2)), rims_cm[:atmos_local], ocean_cm[:, :, :early]]
    )
    atmos_pad = placed([(atmos_int, interior_spots(0, pixels)), (atmos_rims, rim_spots())])
    atmos_accum = conv_cm(atmos_weight, atmos_pad)
    atmos_next = (
        atmos_state.astype(jnp.float32) + jax.nn.gelu(trim_columns(atmos_accum), approximate=True)
    ).astype(jnp.bfloat16)

    sea_rims = jnp.transpose(rims_cm[atmos_local:], (1, 0, 2))
    late_block = jnp.concatenate(
        [atmos_next.reshape(per_dev, -1), sea_rims.reshape(per_dev, -1)], axis=1
    )
    pair_late = pair_order(late_block, partner(late_block, "tiles", 0), parity)
    force_width = atmos_local * pixels
    forcing_cm = pick(
        own_pick, pair_late[:, :force_width].reshape(2 * per_dev, atmos_local, pixels), "st,tcp->csp"
    )
    own_rims_cm = pick(
        own_pick, pair_late[:, force_width:].reshape(2 * per_dev, ocean_local, 4 * SIDE), "st,tcp->csp"
    )

    ocean_tail, ocean_rims, force_all = gather_rows(
        [ocean_cm[:, :, early:], own_rims_cm, forcing_cm]
    )
    ocean_pad = placed(
        [
            (ocean_head, interior_spots(0, early)),
            (ocean_tail, interior_spots(early, pixels - early)),
            (ocean_rims, rim_spots()),
        ]
    )
    conv_accum = conv_cm(ocean_weight, ocean_pad)
    couple_accum = jnp.einsum(
        "oc,cbp->bop", couple_weight, force_all, preferred_element_type=jnp.float32
    )
    mixed = trim_columns(conv_accum) + couple_accum
    ocean_next = (own_ocean.astype(jnp.float32) + jax.nn.gelu(mixed, approximate=True)).astype(
        jnp.bfloat16
    )
    return (atmos_next, ocean_next)


def solution(mesh):
    placed = (
        P("tiles", "chan", None),
        P("tiles", "chan", None),
        P(None, "chan", None),
        P(None, "chan", None),
        P("chan", None),
        P(),
        P(),
        P(),
    )
    return jax.shard_map(
        local,
        mesh=mesh,
        in_specs=placed,
        out_specs=(P("tiles", "chan", None), P("tiles", "chan", None)),
        check_vma=False,
    )
```

```python
import jax
import jax.numpy as jnp
from jax import lax
from jax.sharding import PartitionSpec as P

SIDE = 16


def padded_2(cells, sides, width):
    for axis, dim in sides:
        count = lax.axis_size(axis)
        head = lax.slice_in_dim(cells, 0, width, axis=dim)
        tail = lax.slice_in_dim(cells, cells.shape[dim] - width, cells.shape[dim], axis=dim)
        cells = jnp.concatenate(
            [
                lax.ppermute(tail, axis, [(i, (i + 1) % count) for i in range(count)]),
                cells,
                lax.ppermute(head, axis, [((i + 1) % count, i) for i in range(count)]),
            ],
            axis=dim,
        )
    return cells


def partner(value, axis, distance):
    mask = 2**distance
    pairs = [(source, source ^ mask) for source in range(lax.axis_size(axis))]
    return lax.ppermute(value, axis, pairs)


def edge_set(tile_field):
    tile_count, chan_count = (tile_field.shape[0], tile_field.shape[1])
    tile_grid = tile_field.reshape(tile_count, chan_count, SIDE, SIDE)
    return jnp.stack(
        [
            tile_grid[:, :, 0, :],
            tile_grid[:, :, :, SIDE - 1],
            tile_grid[:, :, SIDE - 1, :],
            tile_grid[:, :, :, 0],
        ],
        axis=2,
    )


def pick_rims(edge_strips, adjacent, turn_codes):
    picked = edge_strips[adjacent]
    side_index = turn_codes % 4
    chosen = picked[:, :, :, 0, :]
    for edge_id in range(1, 4):
        chosen = jnp.where(
            (side_index == edge_id)[:, :, None, None], picked[:, :, :, edge_id, :], chosen
        )
    return jnp.where((turn_codes >= 4)[:, :, None, None], chosen[..., ::-1], chosen)


def pad_tile(tile_field, rim_cells):
    tile_count, chan_count = (tile_field.shape[0], tile_field.shape[1])
    tile_grid = tile_field.reshape(tile_count, chan_count, SIDE, SIDE)
    upper_row = jnp.pad(rim_cells[:, 0], ((0, 0), (0, 0), (1, 1)))[:, :, None, :]
    bottom = jnp.pad(rim_cells[:, 2], ((0, 0), (0, 0), (1, 1)))[:, :, None, :]
    middle = jnp.concatenate(
        [rim_cells[:, 3][:, :, :, None], tile_grid, rim_cells[:, 1][:, :, :, None]], axis=3
    )
    assembled = jnp.concatenate([upper_row, middle, bottom], axis=2).reshape(
        tile_count, chan_count, (SIDE + 2) * (SIDE + 2)
    )
    return jnp.pad(assembled, ((0, 0), (0, 0), (0, 2)))


def trim_columns(accum):
    tile_count, chan_count = (accum.shape[0], accum.shape[1])
    return accum.reshape(tile_count, chan_count, SIDE, SIDE + 2)[:, :, :, :SIDE].reshape(
        tile_count, chan_count, SIDE * SIDE
    )


def conv_step(weight, accum, piece):
    row_width = SIDE + 2
    out_span = SIDE * row_width
    for tap_index in range(9):
        offset = tap_index // 3 * row_width + tap_index % 3
        accum = accum + jnp.einsum(
            "oc,bcp->bop",
            weight[tap_index],
            piece[:, :, offset : offset + out_span],
            preferred_element_type=jnp.float32,
        )
    return accum


def gather_rows(pieces):
    flat = jnp.concatenate([piece.reshape(-1) for piece in pieces])
    rows = flat.reshape(-1, SIDE * SIDE)
    gathered = lax.all_gather(rows, "chan", axis=0, tiled=False)
    groups = gathered.shape[0]
    gathered = gathered.reshape(groups, -1)
    parts = []
    offset = 0
    for piece in pieces:
        size = piece.size
        part = gathered[:, offset : offset + size]
        parts.append(part.reshape((groups * piece.shape[0],) + piece.shape[1:]))
        offset += size
    return parts


def place_matrix(spots, width):
    columns = lax.broadcasted_iota(jnp.int32, (spots.shape[0], width), 1)
    return (columns == spots[:, None]).astype(jnp.bfloat16)


def interior_spots(first, count):
    pixel = jnp.arange(first, first + count, dtype=jnp.int32)
    return (pixel // SIDE + 1) * (SIDE + 2) + pixel % SIDE + 1


def rim_spots():
    k = jnp.arange(SIDE, dtype=jnp.int32) + 1
    row = SIDE + 2
    return jnp.concatenate([k, k * row + SIDE + 1, (SIDE + 1) * row + k, k * row])


def placed(pieces):
    width = (SIDE + 2) * (SIDE + 2) + 2
    total = None
    for piece, spots in pieces:
        term = jnp.einsum(
            "cbq,qp->bcp", piece, place_matrix(spots, width), preferred_element_type=jnp.float32
        )
        total = term if total is None else total + term
    return total.astype(jnp.bfloat16)


def conv_cm(weight, padded):
    row_width = SIDE + 2
    out_span = SIDE * row_width
    taps, out_chans, in_chans = weight.shape
    rows = -(-out_chans // 8) * 8
    weight = jnp.pad(weight, ((0, 0), (0, rows - out_chans), (0, 0)))
    tile_count = padded.shape[0]
    products = jnp.einsum(
        "kc,bcp->bkp",
        weight.reshape(taps * rows, in_chans),
        padded,
        preferred_element_type=jnp.float32,
    ).reshape(tile_count, taps, rows, padded.shape[2])
    accum = None
    for tap_index in range(taps):
        offset = tap_index // 3 * row_width + tap_index % 3
        term = products[:, tap_index, :out_chans, offset : offset + out_span]
        accum = term if accum is None else accum + term
    return accum


def pick(selector, values, spec):
    return jnp.einsum(spec, selector, values, preferred_element_type=jnp.float32).astype(
        jnp.bfloat16
    )


def edge_matrix():
    k = jnp.arange(SIDE, dtype=jnp.int32)
    spots = jnp.concatenate([k, k * SIDE + SIDE - 1, (SIDE - 1) * SIDE + k, k * SIDE])
    rows = lax.broadcasted_iota(jnp.int32, (SIDE * SIDE, 4 * SIDE), 0)
    return (rows == spots[None, :]).astype(jnp.bfloat16)


def pair_order(own, other, parity):
    even = jnp.where(parity == 0, own, other)
    odd = jnp.where(parity == 0, other, own)
    return jnp.concatenate([even, odd], axis=0)


def local(
    atmos_state,
    ocean_state,
    atmos_weight,
    ocean_weight,
    couple_weight,
    sea_mask,
    neighbours,
    rotations,
):
    per_dev = atmos_state.shape[0]
    atmos_local = atmos_state.shape[1]
    ocean_local = ocean_state.shape[1]
    chans = atmos_local + ocean_local
    pixels = SIDE * SIDE
    groups = lax.axis_size("tiles")
    tile_group = lax.axis_index("tiles")
    first_tile = tile_group * per_dev
    per_owner = per_dev * 3 // 4
    parity = tile_group % 2

    both_states = jnp.concatenate([atmos_state, ocean_state], axis=1)
    edges_cm = pick(edge_matrix(), both_states, "qe,bcq->cbe")
    tables = lax.dynamic_slice_in_dim(
        jnp.concatenate([neighbours, rotations, sea_mask[:, None]], axis=1), first_tile, per_dev, 0
    )
    sea_here = tables[:, 8].astype(jnp.bfloat16)
    edges_cm = jnp.concatenate(
        [edges_cm[:atmos_local], edges_cm[atmos_local:] * sea_here[None, :, None]], axis=0
    )
    edge_flat = edges_cm.reshape(-1)
    edge_size = edge_flat.shape[0]
    outgoing = jnp.concatenate([edge_flat, ocean_state.reshape(-1)])
    from_left = lax.ppermute(outgoing, "tiles", [(i, (i + 1) % groups) for i in range(groups)])
    from_right = lax.ppermute(outgoing, "tiles", [((i + 1) % groups, i) for i in range(groups)])

    pair_tiles = 2 * per_dev
    pair_first = tile_group // 2 * pair_tiles
    pair_mask = lax.dynamic_slice_in_dim(sea_mask, pair_first, pair_tiles, 0)
    upto = (
        lax.broadcasted_iota(jnp.int32, (pair_tiles, pair_tiles), 1)
        <= lax.broadcasted_iota(jnp.int32, (pair_tiles, pair_tiles), 0)
    )
    pair_count = jnp.sum(jnp.where(upto, pair_mask[None, :], 0), axis=1)
    local_rank = 2 * jnp.arange(per_owner, dtype=jnp.int32) + parity
    pair_index = jnp.sum((pair_count[None, :] <= local_rank[:, None]).astype(jnp.int32), axis=1)
    own_pick = (
        pair_index[:, None] == jnp.arange(pair_tiles, dtype=jnp.int32)[None, :]
    ).astype(jnp.bfloat16)

    adjacent = tables[:, :4]
    turn_codes = tables[:, 4:8]
    local_adjacent = (adjacent // per_dev - tile_group + 1) % groups * per_dev + adjacent % per_dev
    tile_hit = local_adjacent[None, None, :, :] == jnp.arange(3 * per_dev, dtype=jnp.int32)[
        :, None, None, None
    ]
    edge_hit = (turn_codes % 4)[None, None, :, :] == jnp.arange(4, dtype=jnp.int32)[
        None, :, None, None
    ]
    rim_pick = (tile_hit & edge_hit).astype(jnp.bfloat16).reshape(3 * per_dev * 4, per_dev * 4)
    flip = (
        lax.broadcasted_iota(jnp.int32, (SIDE, SIDE), 0)
        == SIDE - 1 - lax.broadcasted_iota(jnp.int32, (SIDE, SIDE), 1)
    ).astype(jnp.bfloat16)

    partner_state = jnp.where(parity == 0, from_right[edge_size:], from_left[edge_size:])
    pair_state = pair_order(ocean_state, partner_state.reshape(ocean_state.shape), parity)
    ocean_cm = pick(own_pick, pair_state, "st,tcp->csp")
    own_ocean = pick(own_pick, pair_state, "st,tcp->scp")

    widened = jnp.concatenate(
        [
            from_left[:edge_size].reshape(edges_cm.shape),
            edges_cm,
            from_right[:edge_size].reshape(edges_cm.shape),
        ],
        axis=1,
    ).reshape(chans, 3 * per_dev * 4, SIDE)
    straight = pick(rim_pick, widened, "xy,cxk->cyk")
    turned = pick(flip, straight, "kj,cyk->cyj")
    reverse = (turn_codes >= 4).reshape(-1)
    rims_cm = jnp.where(reverse[None, :, None], turned, straight).reshape(chans, per_dev, 4 * SIDE)

    early = 2 * SIDE
    atmos_int, atmos_rims, ocean_head = gather_rows(
        [jnp.transpose(atmos_state, (1, 0, 2)), rims_cm[:atmos_local], ocean_cm[:, :, :early]]
    )
    atmos_pad = placed([(atmos_int, interior_spots(0, pixels)), (atmos_rims, rim_spots())])
    atmos_accum = conv_cm(atmos_weight, atmos_pad)
    atmos_next = (
        atmos_state.astype(jnp.float32) + jax.nn.gelu(trim_columns(atmos_accum), approximate=True)
    ).astype(jnp.bfloat16)

    sea_rims = jnp.transpose(rims_cm[atmos_local:], (1, 0, 2))
    late_block = jnp.concatenate(
        [atmos_next.reshape(per_dev, -1), sea_rims.reshape(per_dev, -1)], axis=1
    )
    pair_late = pair_order(late_block, partner(late_block, "tiles", 0), parity)
    force_width = atmos_local * pixels
    forcing_cm = pick(
        own_pick, pair_late[:, :force_width].reshape(2 * per_dev, atmos_local, pixels), "st,tcp->csp"
    )
    own_rims_cm = pick(
        own_pick, pair_late[:, force_width:].reshape(2 * per_dev, ocean_local, 4 * SIDE), "st,tcp->csp"
    )

    ocean_tail, ocean_rims, force_rows = gather_rows(
        [ocean_cm[:, :, early:], own_rims_cm, forcing_cm.reshape(-1, pixels)]
    )
    ocean_pad = placed(
        [
            (ocean_head, interior_spots(0, early)),
            (ocean_tail, interior_spots(early, pixels - early)),
            (ocean_rims, rim_spots()),
        ]
    )
    conv_accum = conv_cm(ocean_weight, ocean_pad)
    tile_eye = jnp.eye(per_owner, dtype=couple_weight.dtype)
    couple_rows = (couple_weight[None, :, :, None] * tile_eye[:, None, None, :]).reshape(
        per_owner * couple_weight.shape[0], -1
    )
    couple_accum = jnp.einsum(
        "kr,rp->kp", couple_rows, force_rows, preferred_element_type=jnp.float32
    ).reshape(per_owner, couple_weight.shape[0], pixels)
    mixed = trim_columns(conv_accum) + couple_accum
    ocean_next = (own_ocean.astype(jnp.float32) + jax.nn.gelu(mixed, approximate=True)).astype(
        jnp.bfloat16
    )
    return (atmos_next, ocean_next)


def solution(mesh):
    placed = (
        P("tiles", "chan", None),
        P("tiles", "chan", None),
        P(None, "chan", None),
        P(None, "chan", None),
        P("chan", None),
        P(),
        P(),
        P(),
    )
    return jax.shard_map(
        local,
        mesh=mesh,
        in_specs=placed,
        out_specs=(P("tiles", "chan", None), P("tiles", "chan", None)),
        check_vma=False,
    )
```

```python
import jax
import jax.numpy as jnp
from jax import lax
from jax.sharding import PartitionSpec as P

SIDE = 16


def padded_2(cells, sides, width):
    for axis, dim in sides:
        count = lax.axis_size(axis)
        head = lax.slice_in_dim(cells, 0, width, axis=dim)
        tail = lax.slice_in_dim(cells, cells.shape[dim] - width, cells.shape[dim], axis=dim)
        cells = jnp.concatenate(
            [
                lax.ppermute(tail, axis, [(i, (i + 1) % count) for i in range(count)]),
                cells,
                lax.ppermute(head, axis, [((i + 1) % count, i) for i in range(count)]),
            ],
            axis=dim,
        )
    return cells


def partner(value, axis, distance):
    mask = 2**distance
    pairs = [(source, source ^ mask) for source in range(lax.axis_size(axis))]
    return lax.ppermute(value, axis, pairs)


def edge_set(tile_field):
    tile_count, chan_count = (tile_field.shape[0], tile_field.shape[1])
    tile_grid = tile_field.reshape(tile_count, chan_count, SIDE, SIDE)
    return jnp.stack(
        [
            tile_grid[:, :, 0, :],
            tile_grid[:, :, :, SIDE - 1],
            tile_grid[:, :, SIDE - 1, :],
            tile_grid[:, :, :, 0],
        ],
        axis=2,
    )


def pick_rims(edge_strips, adjacent, turn_codes):
    picked = edge_strips[adjacent]
    side_index = turn_codes % 4
    chosen = picked[:, :, :, 0, :]
    for edge_id in range(1, 4):
        chosen = jnp.where(
            (side_index == edge_id)[:, :, None, None], picked[:, :, :, edge_id, :], chosen
        )
    return jnp.where((turn_codes >= 4)[:, :, None, None], chosen[..., ::-1], chosen)


def pad_tile(tile_field, rim_cells):
    tile_count, chan_count = (tile_field.shape[0], tile_field.shape[1])
    tile_grid = tile_field.reshape(tile_count, chan_count, SIDE, SIDE)
    upper_row = jnp.pad(rim_cells[:, 0], ((0, 0), (0, 0), (1, 1)))[:, :, None, :]
    bottom = jnp.pad(rim_cells[:, 2], ((0, 0), (0, 0), (1, 1)))[:, :, None, :]
    middle = jnp.concatenate(
        [rim_cells[:, 3][:, :, :, None], tile_grid, rim_cells[:, 1][:, :, :, None]], axis=3
    )
    assembled = jnp.concatenate([upper_row, middle, bottom], axis=2).reshape(
        tile_count, chan_count, (SIDE + 2) * (SIDE + 2)
    )
    return jnp.pad(assembled, ((0, 0), (0, 0), (0, 2)))


def trim_columns(accum):
    tile_count, chan_count = (accum.shape[0], accum.shape[1])
    return accum.reshape(tile_count, chan_count, SIDE, SIDE + 2)[:, :, :, :SIDE].reshape(
        tile_count, chan_count, SIDE * SIDE
    )


def conv_step(weight, accum, piece):
    row_width = SIDE + 2
    out_span = SIDE * row_width
    for tap_index in range(9):
        offset = tap_index // 3 * row_width + tap_index % 3
        accum = accum + jnp.einsum(
            "oc,bcp->bop",
            weight[tap_index],
            piece[:, :, offset : offset + out_span],
            preferred_element_type=jnp.float32,
        )
    return accum


def gather_rows(pieces):
    flat = jnp.concatenate([piece.reshape(-1) for piece in pieces])
    rows = flat.reshape(-1, SIDE * SIDE)
    gathered = lax.all_gather(rows, "chan", axis=0, tiled=False)
    groups = gathered.shape[0]
    gathered = gathered.reshape(groups, -1)
    parts = []
    offset = 0
    for piece in pieces:
        size = piece.size
        part = gathered[:, offset : offset + size]
        parts.append(part.reshape((groups * piece.shape[0],) + piece.shape[1:]))
        offset += size
    return parts


def place_matrix(spots, width):
    columns = lax.broadcasted_iota(jnp.int32, (spots.shape[0], width), 1)
    return (columns == spots[:, None]).astype(jnp.bfloat16)


def interior_spots(first, count):
    pixel = jnp.arange(first, first + count, dtype=jnp.int32)
    return (pixel // SIDE + 1) * (SIDE + 2) + pixel % SIDE + 1


def rim_spots():
    k = jnp.arange(SIDE, dtype=jnp.int32) + 1
    row = SIDE + 2
    return jnp.concatenate([k, k * row + SIDE + 1, (SIDE + 1) * row + k, k * row])


def placed(pieces):
    width = (SIDE + 2) * (SIDE + 2) + 2
    total = None
    for piece, spots in pieces:
        term = jnp.einsum(
            "cbq,qp->bcp", piece, place_matrix(spots, width), preferred_element_type=jnp.float32
        )
        total = term if total is None else total + term
    return total.astype(jnp.bfloat16)


def conv_cm(weight, padded):
    row_width = SIDE + 2
    out_span = SIDE * row_width
    taps, out_chans, in_chans = weight.shape
    rows = -(-out_chans // 8) * 8
    weight = jnp.pad(weight, ((0, 0), (0, rows - out_chans), (0, 0)))
    tile_count = padded.shape[0]
    products = jnp.einsum(
        "kc,bcp->bkp",
        weight.reshape(taps * rows, in_chans),
        padded,
        preferred_element_type=jnp.float32,
    ).reshape(tile_count, taps, rows, padded.shape[2])
    accum = None
    for tap_index in range(taps):
        offset = tap_index // 3 * row_width + tap_index % 3
        term = products[:, tap_index, :out_chans, offset : offset + out_span]
        accum = term if accum is None else accum + term
    return accum


def pick(selector, values, spec):
    return jnp.einsum(spec, selector, values, preferred_element_type=jnp.float32).astype(
        jnp.bfloat16
    )


def edge_matrix():
    k = jnp.arange(SIDE, dtype=jnp.int32)
    spots = jnp.concatenate([k, k * SIDE + SIDE - 1, (SIDE - 1) * SIDE + k, k * SIDE])
    rows = lax.broadcasted_iota(jnp.int32, (SIDE * SIDE, 4 * SIDE), 0)
    return (rows == spots[None, :]).astype(jnp.bfloat16)


def pair_order(own, other, parity):
    even = jnp.where(parity == 0, own, other)
    odd = jnp.where(parity == 0, other, own)
    return jnp.concatenate([even, odd], axis=0)


def local(
    atmos_state,
    ocean_state,
    atmos_weight,
    ocean_weight,
    couple_weight,
    sea_mask,
    neighbours,
    rotations,
):
    per_dev = atmos_state.shape[0]
    atmos_local = atmos_state.shape[1]
    ocean_local = ocean_state.shape[1]
    chans = atmos_local + ocean_local
    pixels = SIDE * SIDE
    groups = lax.axis_size("tiles")
    tile_group = lax.axis_index("tiles")
    first_tile = tile_group * per_dev
    per_owner = per_dev * 3 // 4
    parity = tile_group % 2

    outgoing = jnp.concatenate(
        [atmos_state.reshape(-1, pixels), ocean_state.reshape(-1, pixels)], axis=0
    )
    from_left = lax.ppermute(outgoing, "tiles", [(i, (i + 1) % groups) for i in range(groups)])
    from_right = lax.ppermute(outgoing, "tiles", [((i + 1) % groups, i) for i in range(groups)])
    atmos_rows = per_dev * atmos_local
    tables = lax.dynamic_slice_in_dim(jnp.concatenate([neighbours, rotations], axis=1), first_tile, per_dev, 0)

    pair_tiles = 2 * per_dev
    pair_first = tile_group // 2 * pair_tiles
    pair_mask = lax.dynamic_slice_in_dim(sea_mask, pair_first, pair_tiles, 0)
    upto = (
        lax.broadcasted_iota(jnp.int32, (pair_tiles, pair_tiles), 1)
        <= lax.broadcasted_iota(jnp.int32, (pair_tiles, pair_tiles), 0)
    )
    pair_count = jnp.sum(jnp.where(upto, pair_mask[None, :], 0), axis=1)
    local_rank = 2 * jnp.arange(per_owner, dtype=jnp.int32) + parity
    pair_index = jnp.sum((pair_count[None, :] <= local_rank[:, None]).astype(jnp.int32), axis=1)
    own_pick = (
        pair_index[:, None] == jnp.arange(pair_tiles, dtype=jnp.int32)[None, :]
    ).astype(jnp.bfloat16)

    adjacent = tables[:, :4]
    turn_codes = tables[:, 4:8]
    rim_mask = sea_mask[adjacent].astype(jnp.bfloat16).reshape(-1)
    local_adjacent = (adjacent // per_dev - tile_group + 1) % groups * per_dev + adjacent % per_dev
    tile_hit = local_adjacent[None, None, :, :] == jnp.arange(3 * per_dev, dtype=jnp.int32)[
        :, None, None, None
    ]
    edge_hit = (turn_codes % 4)[None, None, :, :] == jnp.arange(4, dtype=jnp.int32)[
        None, :, None, None
    ]
    rim_pick = (tile_hit & edge_hit).astype(jnp.bfloat16).reshape(3 * per_dev * 4, per_dev * 4)
    flip = (
        lax.broadcasted_iota(jnp.int32, (SIDE, SIDE), 0)
        == SIDE - 1 - lax.broadcasted_iota(jnp.int32, (SIDE, SIDE), 1)
    ).astype(jnp.bfloat16)

    partner_state = jnp.where(parity == 0, from_right[atmos_rows:], from_left[atmos_rows:])
    pair_state = pair_order(ocean_state, partner_state.reshape(ocean_state.shape), parity)
    ocean_cm = pick(own_pick, pair_state, "st,tcp->csp")
    own_ocean = pick(own_pick, pair_state, "st,tcp->scp")

    edge_pick = edge_matrix()
    wide_atmos = jnp.concatenate(
        [from_left[:atmos_rows], atmos_state.reshape(-1, pixels), from_right[:atmos_rows]], axis=0
    ).reshape(3 * per_dev, atmos_local, pixels)
    wide_ocean = jnp.concatenate(
        [from_left[atmos_rows:], ocean_state.reshape(-1, pixels), from_right[atmos_rows:]], axis=0
    ).reshape(3 * per_dev, ocean_local, pixels)
    widened = jnp.concatenate(
        [pick(edge_pick, wide_atmos, "qe,bcq->cbe"), pick(edge_pick, wide_ocean, "qe,bcq->cbe")], axis=0
    ).reshape(chans, 3 * per_dev * 4, SIDE)
    straight = pick(rim_pick, widened, "xy,cxk->cyk")
    turned = pick(flip, straight, "kj,cyk->cyj")
    reverse = (turn_codes >= 4).reshape(-1)
    rims_cm = jnp.where(reverse[None, :, None], turned, straight)
    rims_cm = jnp.concatenate(
        [rims_cm[:atmos_local], rims_cm[atmos_local:] * rim_mask[None, :, None]], axis=0
    ).reshape(chans, per_dev, 4 * SIDE)

    early = 2 * SIDE
    atmos_int, atmos_rims, ocean_head = gather_rows(
        [jnp.transpose(atmos_state, (1, 0, 2)), rims_cm[:atmos_local], ocean_cm[:, :, :early]]
    )
    atmos_pad = placed([(atmos_int, interior_spots(0, pixels)), (atmos_rims, rim_spots())])
    atmos_accum = conv_cm(atmos_weight, atmos_pad)
    atmos_next = (
        atmos_state.astype(jnp.float32) + jax.nn.gelu(trim_columns(atmos_accum), approximate=True)
    ).astype(jnp.bfloat16)

    sea_rims = jnp.transpose(rims_cm[atmos_local:], (1, 0, 2))
    late_block = jnp.concatenate(
        [atmos_next.reshape(per_dev, -1), sea_rims.reshape(per_dev, -1)], axis=1
    )
    pair_late = pair_order(late_block, partner(late_block, "tiles", 0), parity)
    force_width = atmos_local * pixels
    forcing_cm = pick(
        own_pick, pair_late[:, :force_width].reshape(2 * per_dev, atmos_local, pixels), "st,tcp->csp"
    )
    own_rims_cm = pick(
        own_pick, pair_late[:, force_width:].reshape(2 * per_dev, ocean_local, 4 * SIDE), "st,tcp->csp"
    )

    ocean_tail, ocean_rims, force_all = gather_rows(
        [ocean_cm[:, :, early:], own_rims_cm, forcing_cm]
    )
    ocean_pad = placed(
        [
            (ocean_head, interior_spots(0, early)),
            (ocean_tail, interior_spots(early, pixels - early)),
            (ocean_rims, rim_spots()),
        ]
    )
    conv_accum = conv_cm(ocean_weight, ocean_pad)
    couple_accum = jnp.einsum(
        "oc,cbp->bop", couple_weight, force_all, preferred_element_type=jnp.float32
    )
    mixed = trim_columns(conv_accum) + couple_accum
    ocean_next = (own_ocean.astype(jnp.float32) + jax.nn.gelu(mixed, approximate=True)).astype(
        jnp.bfloat16
    )
    return (atmos_next, ocean_next)


def solution(mesh):
    placed = (
        P("tiles", "chan", None),
        P("tiles", "chan", None),
        P(None, "chan", None),
        P(None, "chan", None),
        P("chan", None),
        P(),
        P(),
        P(),
    )
    return jax.shard_map(
        local,
        mesh=mesh,
        in_specs=placed,
        out_specs=(P("tiles", "chan", None), P("tiles", "chan", None)),
        check_vma=False,
    )
```
